256 devices in a mesh: gx: 8 (over y, core), gy: 16 (over x_lo, z), src: 2 (over x_hi).
Axes of the slice: x: 4 (x_hi: 2, x_lo: 2; x = x_hi * 2 + x_lo), y: 4, z: 8, core: 2. Of those that a mesh axis runs over, the one named last changes fastest.
Arguments:
- conductivity: float32 [16, 128, 128], P('gx', 'gy'), may hold values from 0.3 to 3
- electrodes: int32 [128, 2], replicated, may hold values from 0 to 262143
- pair_order: int32 [128], P('src'), may hold values from 0 to 127, each once
- initial_fields: float32 [128, 16, 128, 128], P('src', 'gx', 'gy'), as said below
- adjoint_fields: float32 [128, 16, 128, 128], P('src', 'gx', 'gy'), may hold values from -6 to 6
Outputs:
- potentials: float32 [128, 16, 128, 128], P('src', 'gx', 'gy')
- gradient: float32 [16, 128, 128], P('gx', 'gy', 'src')
The draws below stay inside these ranges and needn't reach their ends.
Inputs may be any that keep to these rules, and one draw needn't show every extreme that they name: `electrodes`: flat cell index (x * 128 + y) * 128 + z. `pair_order`: each pair appears once. `initial_fields`: every entry lies within 6 / sqrt(262144) in magnitude.
All inputs are finite; a program needn't handle non-finite values.
Results may differ from the reference program's by a relative error of at most 0.00029.
Values sent between devices are 32-bit elements; how exact they have to be, the bound alone decides.
No kernel may reach another device: no remote copies, remote signals or barrier semaphores. Data moves between devices by JAX's collectives and lax.ppermute only.
A program may use at most 64 MiB of HBM per device.

```python
import math
import jax
import jax.numpy as jnp
from jax import lax

COLS = 64
ITERS = 2
NX = 16
NY = 128
NZ = 128
PAIRS = 128
N_SRC = 2


def draw_initial_fields(key, part):
    spread = 1.0 / math.sqrt(NX * NY * NZ)
    values = jnp.clip(jax.random.normal(key, (PAIRS, NX, NY, NZ), jnp.float32), -6.0, 6.0)
    return (values * spread).astype(jnp.float32)


def plant(array, rng, smallest, top_value):
    index_at = [jax.random.randint(jax.random.fold_in(rng, axis), (), 0, length) for axis, length in enumerate(array.shape)]
    main_axis = array.shape.index(max(array.shape))
    neighbour = index_at[:main_axis] + [(index_at[main_axis] + 1) % array.shape[main_axis]] + index_at[main_axis + 1:]
    return array.at[tuple(index_at)].set(smallest).at[tuple(neighbour)].set(top_value)


def shard_levels(stream_key, dims, shards, smallest, largest):
    loudness, own = 1.0, jax.random.fold_in(stream_key, 6)
    for dim, blocks in shards:
        steps = jnp.exp(jax.random.uniform(jax.random.fold_in(own, dim), (blocks,), jnp.float32, smallest / len(shards), largest / len(shards)))
        loudness = loudness * jnp.repeat(steps, dims[dim] // blocks).reshape([-1 if axis == dim else 1 for axis in range(len(dims))])
    return loudness


def normal_values(own_key, dims, scale, limit, cuts=(), kind=jnp.bfloat16):
    drawn = scale * jax.random.normal(own_key, dims, jnp.float32)
    if cuts:
        drawn = drawn * shard_levels(own_key, dims, cuts, -0.22, 0.18)
    return jnp.clip(drawn, -limit, limit).astype(kind)


def setup_inputs(seed: int = 0) -> dict:
    key_of = jax.random.split(jax.random.key(seed), 6)
    conductivity = jnp.clip(jnp.exp(math.log(3.0) - 2.3025851 * jax.random.uniform(key_of[0], (NX, NY, NZ), jnp.float32) ** shard_levels(key_of[0], (NX, NY, NZ), ((0, 8), (1, 16)), -0.2, 0.2)), 0.3, 3.0)
    electrodes = plant(jax.random.randint(key_of[1], (PAIRS, 2), 0, NX * NY * NZ), jax.random.fold_in(key_of[1], 1), 0, (NX * NY * NZ) - 1).astype(jnp.int32)
    pair_order = jax.random.permutation(key_of[2], PAIRS).astype(jnp.int32)
    initial_fields = draw_initial_fields(jax.random.fold_in(key_of[5], 71), 0)
    adjoint_fields = normal_values(key_of[4], (PAIRS, NX, NY, NZ), 1.0, 6.0, ((0, 2), (1, 8), (2, 16)), jnp.float32)
    return dict(conductivity=conductivity, electrodes=electrodes, pair_order=pair_order, initial_fields=initial_fields, adjoint_fields=adjoint_fields)


INJECT = 4.0

def conductances(sigma):
    full = jnp.pad(sigma, 1)
    cond_x = 0.5 * (full[1:, 1:-1, 1:-1] + full[:-1, 1:-1, 1:-1])
    cond_y = 0.5 * (full[1:-1, 1:, 1:-1] + full[1:-1, :-1, 1:-1])
    cond_z = 0.5 * (full[1:-1, 1:-1, 1:] + full[1:-1, 1:-1, :-1])
    return (cond_x, cond_y, cond_z)

def operator(field, conds):
    full = jnp.pad(field, ((0, 0), (1, 1), (1, 1), (1, 1)))
    flux_x = conds[0] * (full[:, 1:, 1:-1, 1:-1] - full[:, :-1, 1:-1, 1:-1])
    flux_y = conds[1] * (full[:, 1:-1, 1:, 1:-1] - full[:, 1:-1, :-1, 1:-1])
    flux_z = conds[2] * (full[:, 1:-1, 1:-1, 1:] - full[:, 1:-1, 1:-1, :-1])
    return flux_x[:, :-1] - flux_x[:, 1:] + (flux_y[:, :, :-1] - flux_y[:, :, 1:]) + (flux_z[..., :-1] - flux_z[..., 1:])

def gram_of(left, right):
    return jnp.einsum('axyz,bxyz->ab', left, right, precision=lax.Precision.HIGHEST)

def combine_cols(field, matrix):
    return jnp.einsum('axyz,ab->bxyz', field, matrix, precision=lax.Precision.HIGHEST)

def posdef_solve(matrix, right):
    lower = jnp.linalg.cholesky(matrix)
    middle = lax.linalg.triangular_solve(lower, right, left_side=True, lower=True)
    return lax.linalg.triangular_solve(lower, middle, left_side=True, lower=True, transpose_a=True)

def one_hot(cells, count):
    return (cells[:, None] == jnp.arange(count, dtype=jnp.int32)[None, :]).astype(jnp.float32)

def point_source(flat):
    xs = flat // (NY * NZ)
    ys = flat // NZ % NY
    zs = flat % NZ
    return jnp.einsum('cx,cy,cz->cxyz', one_hot(xs, NX), one_hot(ys, NY), one_hot(zs, NZ))

def reference(conductivity, electrodes, pair_order, initial_fields, adjoint_fields):
    conds = conductances(conductivity)
    results = []
    gradient = jnp.zeros((NX, NY, NZ), jnp.float32)
    for group_index in range(N_SRC):
        first = group_index * COLS
        picked = electrodes[pair_order[first:first + COLS]]
        right = INJECT * (point_source(picked[:, 0]) - point_source(picked[:, 1]))
        iterate = initial_fields[first:first + COLS]
        adjoint = adjoint_fields[first:first + COLS]
        residual = right - operator(iterate, conds)
        direction = residual
        res_gram = gram_of(residual, residual)
        for iteration in range(ITERS):
            image = operator(direction, conds)
            curv_gram = gram_of(direction, image)
            step_mat = posdef_solve(curv_gram, res_gram)
            iterate = iterate + combine_cols(direction, step_mat)
            residual = residual - combine_cols(image, step_mat)
            if iteration + 1 < ITERS:
                new_gram = gram_of(residual, residual)
                turn_mat = posdef_solve(res_gram, new_gram)
                direction = residual + combine_cols(direction, turn_mat)
                res_gram = new_gram
        results.append(iterate)
        fu = jnp.pad(iterate, ((0, 0), (1, 1), (1, 1), (1, 1)))
        fl = jnp.pad(adjoint, ((0, 0), (1, 1), (1, 1), (1, 1)))
        term_x = jnp.sum((fu[:, 1:, 1:-1, 1:-1] - fu[:, :-1, 1:-1, 1:-1]) * (fl[:, 1:, 1:-1, 1:-1] - fl[:, :-1, 1:-1, 1:-1]), axis=0)
        term_y = jnp.sum((fu[:, 1:-1, 1:, 1:-1] - fu[:, 1:-1, :-1, 1:-1]) * (fl[:, 1:-1, 1:, 1:-1] - fl[:, 1:-1, :-1, 1:-1]), axis=0)
        term_z = jnp.sum((fu[:, 1:-1, 1:-1, 1:] - fu[:, 1:-1, 1:-1, :-1]) * (fl[:, 1:-1, 1:-1, 1:] - fl[:, 1:-1, 1:-1, :-1]), axis=0)
        gradient = gradient + -0.5 / COLS * (term_x[:-1] + term_x[1:] + term_y[:, :-1] + term_y[:, 1:] + term_z[..., :-1] + term_z[..., 1:])
    return (jnp.concatenate(results, axis=0), gradient)
```

```python
import jax
import jax.numpy as jnp
from jax import lax
from jax.sharding import PartitionSpec as P

ITERS = 2


INJECT = 4.0


def padded_2(block, sides, width):
    (axis_x, dim_x), (axis_y, dim_y) = sides
    pieces = {}
    for axis, dim in sides:
        count = lax.axis_size(axis)
        forward = [(i, i + 1) for i in range(count - 1)]
        backward = [(target, source) for source, target in forward]
        low = lax.ppermute(
            lax.slice_in_dim(block, block.shape[dim] - width, None, axis=dim), axis, forward
        )
        high = lax.ppermute(lax.slice_in_dim(block, 0, width, axis=dim), axis, backward)
        pieces[axis] = (low, high)
    low_x, high_x = pieces[axis_x]
    low_y, high_y = pieces[axis_y]
    middle = jnp.concatenate([low_x, block, high_x], axis=dim_x)
    rim = [(0, 0)] * block.ndim
    rim[dim_x] = (width, width)
    low_y = jnp.pad(low_y, rim)
    high_y = jnp.pad(high_y, rim)
    return jnp.concatenate([low_y, middle, high_y], axis=dim_y)


def allsum(value, axes):
    for axis in axes:
        count = lax.axis_size(axis)
        if count & (count - 1):
            value = lax.psum(value, axis)
            continue
        step = 1
        while step < count:
            pairs = [(i, i ^ step) for i in range(count)]
            value = value + lax.ppermute(value, axis, pairs)
            step *= 2
    return value


def conductances(sig_pad):
    full = jnp.pad(sig_pad, ((0, 0), (0, 0), (1, 1)))
    cond_x = 0.5 * (full[1:, 1:-1, 1:-1] + full[:-1, 1:-1, 1:-1])
    cond_y = 0.5 * (full[1:-1, 1:, 1:-1] + full[1:-1, :-1, 1:-1])
    cond_z = 0.5 * (full[1:-1, 1:-1, 1:] + full[1:-1, 1:-1, :-1])
    return (cond_x, cond_y, cond_z)


def operator(padded, conds):
    full = jnp.pad(padded, ((0, 0), (0, 0), (0, 0), (1, 1)))
    flux_x = conds[0] * (full[:, 1:, 1:-1, 1:-1] - full[:, :-1, 1:-1, 1:-1])
    flux_y = conds[1] * (full[:, 1:-1, 1:, 1:-1] - full[:, 1:-1, :-1, 1:-1])
    flux_z = conds[2] * (full[:, 1:-1, 1:-1, 1:] - full[:, 1:-1, 1:-1, :-1])
    return (
        flux_x[:, :-1]
        - flux_x[:, 1:]
        + (flux_y[:, :, :-1] - flux_y[:, :, 1:])
        + (flux_z[..., :-1] - flux_z[..., 1:])
    )


def gram_of(left, right):
    return jnp.einsum("axyz,bxyz->ab", left, right, precision=lax.Precision.HIGHEST)


def combine_cols(field, matrix):
    return jnp.einsum("axyz,ab->bxyz", field, matrix, precision=lax.Precision.HIGHEST)


def posdef_solve(matrix, right):
    lower = jnp.linalg.cholesky(matrix)
    middle = lax.linalg.triangular_solve(lower, right, left_side=True, lower=True)
    return lax.linalg.triangular_solve(lower, middle, left_side=True, lower=True, transpose_a=True)


def one_hot(cells, start, count):
    return (cells[:, None] == start + jnp.arange(count, dtype=jnp.int32)[None, :]).astype(
        jnp.float32
    )


def face_terms(field_pad, adjoint_pad):
    fu = jnp.pad(field_pad, ((0, 0), (0, 0), (0, 0), (1, 1)))
    fl = jnp.pad(adjoint_pad, ((0, 0), (0, 0), (0, 0), (1, 1)))
    term_x = jnp.sum(
        (fu[:, 1:, 1:-1, 1:-1] - fu[:, :-1, 1:-1, 1:-1])
        * (fl[:, 1:, 1:-1, 1:-1] - fl[:, :-1, 1:-1, 1:-1]),
        axis=0,
    )
    term_y = jnp.sum(
        (fu[:, 1:-1, 1:, 1:-1] - fu[:, 1:-1, :-1, 1:-1])
        * (fl[:, 1:-1, 1:, 1:-1] - fl[:, 1:-1, :-1, 1:-1]),
        axis=0,
    )
    term_z = jnp.sum(
        (fu[:, 1:-1, 1:-1, 1:] - fu[:, 1:-1, 1:-1, :-1])
        * (fl[:, 1:-1, 1:-1, 1:] - fl[:, 1:-1, 1:-1, :-1]),
        axis=0,
    )
    return (term_x, term_y, term_z)


def on_device(conductivity, electrodes, pair_order, initial_fields, adjoint_fields):
    cells_x, cells_y, cells_z = conductivity.shape
    columns = initial_fields.shape[0]
    total_y = lax.axis_size("gy") * cells_y
    start_x = lax.axis_index("gx") * cells_x
    start_y = lax.axis_index("gy") * cells_y
    picked = jnp.take(electrodes, pair_order, axis=0)

    def point_source(flat):
        xs = flat // (total_y * cells_z)
        ys = flat // cells_z % total_y
        zs = flat % cells_z
        return jnp.einsum(
            "cx,cy,cz->cxyz",
            one_hot(xs, start_x, cells_x),
            one_hot(ys, start_y, cells_y),
            one_hot(zs, 0, cells_z),
        )

    right = INJECT * (point_source(picked[:, 0]) - point_source(picked[:, 1]))
    stacked = jnp.concatenate([conductivity[None], initial_fields], axis=0)
    padded = padded_2(stacked, (("gx", 1), ("gy", 2)), 1)
    conds = conductances(padded[0])
    iterate = initial_fields
    iter_pad = padded[1:]
    residual = right - operator(iter_pad, conds)
    grid_axes = ("gx", "gy")
    direction = residual
    res_gram = None
    for iteration in range(ITERS):
        dir_pad = padded_2(direction, (("gx", 1), ("gy", 2)), 1)
        image = operator(dir_pad, conds)
        if res_gram is None:
            grams = allsum(
                jnp.stack([gram_of(residual, residual), gram_of(direction, image)]), grid_axes
            )
            res_gram, curv_gram = grams[0], grams[1]
        else:
            curv_gram = allsum(gram_of(direction, image), grid_axes)
        step_mat = posdef_solve(curv_gram, res_gram)
        iterate = iterate + combine_cols(direction, step_mat)
        residual = residual - combine_cols(image, step_mat)
        if iteration + 1 < ITERS:
            new_gram = allsum(gram_of(residual, residual), grid_axes)
            turn_mat = posdef_solve(res_gram, new_gram)
            direction = residual + combine_cols(direction, turn_mat)
            res_gram = new_gram
    both = jnp.concatenate([iterate, adjoint_fields], axis=0)
    both_pad = padded_2(both, (("gx", 1), ("gy", 2)), 1)
    term_x, term_y, term_z = face_terms(both_pad[:columns], both_pad[columns:])
    local_grad = (
        -0.5
        / columns
        * (
            term_x[:-1]
            + term_x[1:]
            + term_y[:, :-1]
            + term_y[:, 1:]
            + term_z[..., :-1]
            + term_z[..., 1:]
        )
    )
    groups = lax.axis_size("src")
    share = cells_z // groups
    own = lax.axis_index("src")
    if groups == 2:
        other = 1 - own
        sent = lax.dynamic_slice_in_dim(local_grad, other * share, share, 2)
        got = lax.ppermute(sent, "src", [(0, 1), (1, 0)])
        gradient = lax.dynamic_slice_in_dim(local_grad, own * share, share, 2) + got
    else:
        summed = lax.psum(local_grad, "src")
        gradient = lax.dynamic_slice_in_dim(summed, own * share, share, 2)
    return (iterate, gradient)


def solution(mesh):
    placed = (
        P("gx", "gy", None),
        P(),
        P("src"),
        P("src", "gx", "gy", None),
        P("src", "gx", "gy", None),
    )
    return jax.shard_map(
        on_device,
        mesh=mesh,
        in_specs=placed,
        out_specs=(P("src", "gx", "gy", None), P("gx", "gy", "src")),
        check_vma=False,
    )
```

```python
import jax
import jax.numpy as jnp
from jax import lax
from jax.sharding import PartitionSpec as P

ITERS = 2


INJECT = 4.0


def padded_2(block, sides, width):
    (axis_x, dim_x), (axis_y, dim_y) = sides
    pieces = {}
    for axis, dim in sides:
        count = lax.axis_size(axis)
        forward = [(i, i + 1) for i in range(count - 1)]
        backward = [(target, source) for source, target in forward]
        low = lax.ppermute(
            lax.slice_in_dim(block, block.shape[dim] - width, None, axis=dim), axis, forward
        )
        high = lax.ppermute(lax.slice_in_dim(block, 0, width, axis=dim), axis, backward)
        pieces[axis] = (low, high)
    low_x, high_x = pieces[axis_x]
    low_y, high_y = pieces[axis_y]
    middle = jnp.concatenate([low_x, block, high_x], axis=dim_x)
    rim = [(0, 0)] * block.ndim
    rim[dim_x] = (width, width)
    low_y = jnp.pad(low_y, rim)
    high_y = jnp.pad(high_y, rim)
    return jnp.concatenate([low_y, middle, high_y], axis=dim_y)


def allsum(value, axes):
    for axis in axes:
        count = lax.axis_size(axis)
        if count & (count - 1):
            value = lax.psum(value, axis)
            continue
        step = 1
        while step < count:
            pairs = [(i, i ^ step) for i in range(count)]
            value = value + lax.ppermute(value, axis, pairs)
            step *= 2
    return value


def conductances(sig_pad):
    full = jnp.pad(sig_pad, ((0, 0), (0, 0), (1, 1)))
    cond_x = 0.5 * (full[1:, 1:-1, 1:-1] + full[:-1, 1:-1, 1:-1])
    cond_y = 0.5 * (full[1:-1, 1:, 1:-1] + full[1:-1, :-1, 1:-1])
    cond_z = 0.5 * (full[1:-1, 1:-1, 1:] + full[1:-1, 1:-1, :-1])
    return (cond_x, cond_y, cond_z)


def operator(padded, conds):
    full = jnp.pad(padded, ((0, 0), (0, 0), (0, 0), (1, 1)))
    flux_x = conds[0] * (full[:, 1:, 1:-1, 1:-1] - full[:, :-1, 1:-1, 1:-1])
    flux_y = conds[1] * (full[:, 1:-1, 1:, 1:-1] - full[:, 1:-1, :-1, 1:-1])
    flux_z = conds[2] * (full[:, 1:-1, 1:-1, 1:] - full[:, 1:-1, 1:-1, :-1])
    return (
        flux_x[:, :-1]
        - flux_x[:, 1:]
        + (flux_y[:, :, :-1] - flux_y[:, :, 1:])
        + (flux_z[..., :-1] - flux_z[..., 1:])
    )


def gram_of(left, right):
    return jnp.einsum("axyz,bxyz->ab", left, right, precision=lax.Precision.HIGHEST)


def combine_cols(field, matrix):
    return jnp.einsum("axyz,ab->bxyz", field, matrix, precision=lax.Precision.HIGHEST)


def posdef_solve(matrix, right):
    lower = jnp.linalg.cholesky(matrix)
    middle = lax.linalg.triangular_solve(lower, right, left_side=True, lower=True)
    return lax.linalg.triangular_solve(lower, middle, left_side=True, lower=True, transpose_a=True)


def one_hot(cells, start, count):
    return (cells[:, None] == start + jnp.arange(count, dtype=jnp.int32)[None, :]).astype(
        jnp.float32
    )


def face_terms(field_pad, adjoint_pad):
    fu = jnp.pad(field_pad, ((0, 0), (0, 0), (0, 0), (1, 1)))
    fl = jnp.pad(adjoint_pad, ((0, 0), (0, 0), (0, 0), (1, 1)))
    term_x = jnp.sum(
        (fu[:, 1:, 1:-1, 1:-1] - fu[:, :-1, 1:-1, 1:-1])
        * (fl[:, 1:, 1:-1, 1:-1] - fl[:, :-1, 1:-1, 1:-1]),
        axis=0,
    )
    term_y = jnp.sum(
        (fu[:, 1:-1, 1:, 1:-1] - fu[:, 1:-1, :-1, 1:-1])
        * (fl[:, 1:-1, 1:, 1:-1] - fl[:, 1:-1, :-1, 1:-1]),
        axis=0,
    )
    term_z = jnp.sum(
        (fu[:, 1:-1, 1:-1, 1:] - fu[:, 1:-1, 1:-1, :-1])
        * (fl[:, 1:-1, 1:-1, 1:] - fl[:, 1:-1, 1:-1, :-1]),
        axis=0,
    )
    return (term_x, term_y, term_z)


def on_device(conductivity, electrodes, pair_order, initial_fields, adjoint_fields):
    cells_x, cells_y, cells_z = conductivity.shape
    columns = initial_fields.shape[0]
    total_y = lax.axis_size("gy") * cells_y
    start_x = lax.axis_index("gx") * cells_x
    start_y = lax.axis_index("gy") * cells_y
    picked = jnp.take(electrodes, pair_order, axis=0)

    def point_source(flat):
        xs = flat // (total_y * cells_z)
        ys = flat // cells_z % total_y
        zs = flat % cells_z
        return jnp.einsum(
            "cx,cy,cz->cxyz",
            one_hot(xs, start_x, cells_x),
            one_hot(ys, start_y, cells_y),
            one_hot(zs, 0, cells_z),
        )

    right = INJECT * (point_source(picked[:, 0]) - point_source(picked[:, 1]))
    sides = (("gx", 1), ("gy", 2))
    grid_axes = ("gx", "gy")
    stacked = jnp.concatenate([conductivity[None], initial_fields, adjoint_fields], axis=0)
    padded = padded_2(stacked, sides, 1)
    conds = conductances(padded[0])
    iter_pad = padded[1 : 1 + columns]
    adjoint_pad = padded[1 + columns :]
    residual = right - operator(iter_pad, conds)
    res_pad = padded_2(residual, sides, 1)
    image = operator(res_pad, conds)
    image_pad = padded_2(image, sides, 1)
    image2 = operator(image_pad, conds)
    grams = allsum(
        jnp.stack(
            [
                gram_of(residual, residual),
                gram_of(residual, image),
                gram_of(image, image),
                gram_of(image, image2),
            ]
        ),
        grid_axes,
    )
    g_rr, g_rq, g_qq, g_qw = grams[0], grams[1], grams[2], grams[3]

    def mm(left, right):
        return jnp.matmul(left, right, precision=lax.Precision.HIGHEST)

    step0 = posdef_solve(g_rq, g_rr)
    cross = mm(g_rq, step0)
    new_gram = g_rr - cross - cross.T + mm(step0.T, mm(g_qq, step0))
    turn = posdef_solve(g_rr, new_gram)
    keep = jnp.eye(columns, dtype=turn.dtype) + turn
    back = -step0
    curv = (
        mm(keep.T, mm(g_rq, keep))
        + mm(keep.T, mm(g_qq, back))
        + mm(back.T, mm(g_qq, keep))
        + mm(back.T, mm(g_qw, back))
    )
    step1 = posdef_solve(curv, new_gram)
    res1_pad = res_pad - combine_cols(image_pad, step0)
    dir1_pad = res1_pad + combine_cols(res_pad, turn)
    it1_pad = iter_pad + combine_cols(res_pad, step0)
    it2_pad = it1_pad + combine_cols(dir1_pad, step1)
    iterate = it2_pad[:, 1:-1, 1:-1]
    term_x, term_y, term_z = face_terms(it2_pad, adjoint_pad)
    local_grad = (
        -0.5
        / columns
        * (
            term_x[:-1]
            + term_x[1:]
            + term_y[:, :-1]
            + term_y[:, 1:]
            + term_z[..., :-1]
            + term_z[..., 1:]
        )
    )
    groups = lax.axis_size("src")
    share = cells_z // groups
    own = lax.axis_index("src")
    if groups == 2:
        other = 1 - own
        sent = lax.dynamic_slice_in_dim(local_grad, other * share, share, 2)
        got = lax.ppermute(sent, "src", [(0, 1), (1, 0)])
        gradient = lax.dynamic_slice_in_dim(local_grad, own * share, share, 2) + got
    else:
        summed = lax.psum(local_grad, "src")
        gradient = lax.dynamic_slice_in_dim(summed, own * share, share, 2)
    return (iterate, gradient)


def solution(mesh):
    placed = (
        P("gx", "gy", None),
        P(),
        P("src"),
        P("src", "gx", "gy", None),
        P("src", "gx", "gy", None),
    )
    return jax.shard_map(
        on_device,
        mesh=mesh,
        in_specs=placed,
        out_specs=(P("src", "gx", "gy", None), P("gx", "gy", "src")),
        check_vma=False,
    )
```

```python
import jax
import jax.numpy as jnp
from jax import lax
from jax.sharding import PartitionSpec as P
from jax.experimental import pallas as pl

ITERS = 2


INJECT = 4.0


def padded_2(block, sides, width):
    (axis_x, dim_x), (axis_y, dim_y) = sides
    pieces = {}
    for axis, dim in sides:
        count = lax.axis_size(axis)
        forward = [(i, i + 1) for i in range(count - 1)]
        backward = [(target, source) for source, target in forward]
        low = lax.ppermute(
            lax.slice_in_dim(block, block.shape[dim] - width, None, axis=dim), axis, forward
        )
        high = lax.ppermute(lax.slice_in_dim(block, 0, width, axis=dim), axis, backward)
        pieces[axis] = (low, high)
    low_x, high_x = pieces[axis_x]
    low_y, high_y = pieces[axis_y]
    middle = jnp.concatenate([low_x, block, high_x], axis=dim_x)
    rim = [(0, 0)] * block.ndim
    rim[dim_x] = (width, width)
    low_y = jnp.pad(low_y, rim)
    high_y = jnp.pad(high_y, rim)
    return jnp.concatenate([low_y, middle, high_y], axis=dim_y)


def allsum(value, axes):
    for axis in axes:
        count = lax.axis_size(axis)
        if count & (count - 1):
            value = lax.psum(value, axis)
            continue
        step = 1
        while step < count:
            pairs = [(i, i ^ step) for i in range(count)]
            value = value + lax.ppermute(value, axis, pairs)
            step *= 2
    return value


def conductances(sig_pad):
    full = jnp.pad(sig_pad, ((0, 0), (0, 0), (1, 1)))
    cond_x = 0.5 * (full[1:, 1:-1, 1:-1] + full[:-1, 1:-1, 1:-1])
    cond_y = 0.5 * (full[1:-1, 1:, 1:-1] + full[1:-1, :-1, 1:-1])
    cond_z = 0.5 * (full[1:-1, 1:-1, 1:] + full[1:-1, 1:-1, :-1])
    return (cond_x, cond_y, cond_z)


def operator(padded, conds):
    full = jnp.pad(padded, ((0, 0), (0, 0), (0, 0), (1, 1)))
    flux_x = conds[0] * (full[:, 1:, 1:-1, 1:-1] - full[:, :-1, 1:-1, 1:-1])
    flux_y = conds[1] * (full[:, 1:-1, 1:, 1:-1] - full[:, 1:-1, :-1, 1:-1])
    flux_z = conds[2] * (full[:, 1:-1, 1:-1, 1:] - full[:, 1:-1, 1:-1, :-1])
    return (
        flux_x[:, :-1]
        - flux_x[:, 1:]
        + (flux_y[:, :, :-1] - flux_y[:, :, 1:])
        + (flux_z[..., :-1] - flux_z[..., 1:])
    )


def gram_of(left, right):
    return jnp.einsum("axyz,bxyz->ab", left, right, precision=lax.Precision.HIGHEST)


def combine_cols(field, matrix):
    return jnp.einsum("axyz,ab->bxyz", field, matrix, precision=lax.Precision.HIGHEST)


def posdef_solve(matrix, right):
    lower = jnp.linalg.cholesky(matrix)
    middle = lax.linalg.triangular_solve(lower, right, left_side=True, lower=True)
    return lax.linalg.triangular_solve(lower, middle, left_side=True, lower=True, transpose_a=True)


def one_hot(cells, start, count):
    return (cells[:, None] == start + jnp.arange(count, dtype=jnp.int32)[None, :]).astype(
        jnp.float32
    )


def face_terms(field_pad, adjoint_pad):
    fu = jnp.pad(field_pad, ((0, 0), (0, 0), (0, 0), (1, 1)))
    fl = jnp.pad(adjoint_pad, ((0, 0), (0, 0), (0, 0), (1, 1)))
    term_x = jnp.sum(
        (fu[:, 1:, 1:-1, 1:-1] - fu[:, :-1, 1:-1, 1:-1])
        * (fl[:, 1:, 1:-1, 1:-1] - fl[:, :-1, 1:-1, 1:-1]),
        axis=0,
    )
    term_y = jnp.sum(
        (fu[:, 1:-1, 1:, 1:-1] - fu[:, 1:-1, :-1, 1:-1])
        * (fl[:, 1:-1, 1:, 1:-1] - fl[:, 1:-1, :-1, 1:-1]),
        axis=0,
    )
    term_z = jnp.sum(
        (fu[:, 1:-1, 1:-1, 1:] - fu[:, 1:-1, 1:-1, :-1])
        * (fl[:, 1:-1, 1:-1, 1:] - fl[:, 1:-1, 1:-1, :-1]),
        axis=0,
    )
    return (term_x, term_y, term_z)


HI = lax.Precision.HIGHEST

def _mm(a, b):
    return jnp.dot(a, b, precision=HI, preferred_element_type=jnp.float32)

def _tr(a):
    return jnp.transpose(a)

def _solve(matrix, right):
    n = matrix.shape[0]
    rows = lax.broadcasted_iota(jnp.int32, matrix.shape, 0)
    lanes = lax.broadcasted_iota(jnp.int32, matrix.shape, 1)
    lane_r = lax.broadcasted_iota(jnp.int32, (1, n), 1)

    def step(j, carry):
        m, r = carry
        pick = rows == j
        row_m = jnp.sum(jnp.where(pick, m, 0.0), axis=0, keepdims=True)
        row_r = jnp.sum(jnp.where(pick, r, 0.0), axis=0, keepdims=True)
        pivot = jnp.sum(jnp.where(lane_r == j, row_m, 0.0), axis=1, keepdims=True)
        col = jnp.sum(jnp.where(lanes == j, m, 0.0), axis=1, keepdims=True)
        row_m = row_m / pivot
        row_r = row_r / pivot
        m = jnp.where(pick, row_m, m - col * row_m)
        r = jnp.where(pick, row_r, r - col * row_r)
        return m, r

    _, out = lax.fori_loop(0, n, step, (matrix, right))
    return out

def steps_kernel(grams_ref, out_ref):
    g_rr = grams_ref[0]
    g_rq = grams_ref[1]
    g_qq = grams_ref[2]
    g_qw = grams_ref[3]
    n = g_rr.shape[0]
    step0 = _solve(g_rq, g_rr)
    cross = _mm(g_rq, step0)
    step0_t = _tr(step0)
    new_gram = g_rr - cross - _tr(cross) + _mm(step0_t, _mm(g_qq, step0))
    turn = _solve(g_rr, new_gram)
    eye = (lax.broadcasted_iota(jnp.int32, (n, n), 0) == lax.broadcasted_iota(jnp.int32, (n, n), 1)).astype(jnp.float32)
    keep = eye + turn
    keep_t = _tr(keep)
    curv = (_mm(keep_t, _mm(g_rq, keep)) - _mm(keep_t, _mm(g_qq, step0))
            - _mm(step0_t, _mm(g_qq, keep)) + _mm(step0_t, _mm(g_qw, step0)))
    step1 = _solve(curv, new_gram)
    out_ref[0] = step0
    out_ref[1] = turn
    out_ref[2] = step1

def steps(grams):
    n = grams.shape[1]
    return pl.pallas_call(steps_kernel, out_shape=jax.ShapeDtypeStruct((3, n, n), jnp.float32))(grams)


def on_device(conductivity, electrodes, pair_order, initial_fields, adjoint_fields):
    cells_x, cells_y, cells_z = conductivity.shape
    columns = initial_fields.shape[0]
    total_y = lax.axis_size("gy") * cells_y
    start_x = lax.axis_index("gx") * cells_x
    start_y = lax.axis_index("gy") * cells_y
    picked = jnp.take(electrodes, pair_order, axis=0)

    def point_source(flat):
        xs = flat // (total_y * cells_z)
        ys = flat // cells_z % total_y
        zs = flat % cells_z
        return jnp.einsum(
            "cx,cy,cz->cxyz",
            one_hot(xs, start_x, cells_x),
            one_hot(ys, start_y, cells_y),
            one_hot(zs, 0, cells_z),
        )

    right = INJECT * (point_source(picked[:, 0]) - point_source(picked[:, 1]))
    sides = (("gx", 1), ("gy", 2))
    grid_axes = ("gx", "gy")
    stacked = jnp.concatenate([conductivity[None], initial_fields, adjoint_fields], axis=0)
    padded = padded_2(stacked, sides, 1)
    conds = conductances(padded[0])
    iter_pad = padded[1 : 1 + columns]
    adjoint_pad = padded[1 + columns :]
    residual = right - operator(iter_pad, conds)
    res_pad = padded_2(residual, sides, 1)
    image = operator(res_pad, conds)
    image_pad = padded_2(image, sides, 1)
    image2 = operator(image_pad, conds)
    grams = allsum(
        jnp.stack(
            [
                gram_of(residual, residual),
                gram_of(residual, image),
                gram_of(image, image),
                gram_of(image, image2),
            ]
        ),
        grid_axes,
    )

    solved = steps(grams)
    step0, turn, step1 = solved[0], solved[1], solved[2]
    res1_pad = res_pad - combine_cols(image_pad, step0)
    dir1_pad = res1_pad + combine_cols(res_pad, turn)
    it1_pad = iter_pad + combine_cols(res_pad, step0)
    it2_pad = it1_pad + combine_cols(dir1_pad, step1)
    iterate = it2_pad[:, 1:-1, 1:-1]
    term_x, term_y, term_z = face_terms(it2_pad, adjoint_pad)
    local_grad = (
        -0.5
        / columns
        * (
            term_x[:-1]
            + term_x[1:]
            + term_y[:, :-1]
            + term_y[:, 1:]
            + term_z[..., :-1]
            + term_z[..., 1:]
        )
    )
    groups = lax.axis_size("src")
    share = cells_z // groups
    own = lax.axis_index("src")
    if groups == 2:
        other = 1 - own
        sent = lax.dynamic_slice_in_dim(local_grad, other * share, share, 2)
        got = lax.ppermute(sent, "src", [(0, 1), (1, 0)])
        gradient = lax.dynamic_slice_in_dim(local_grad, own * share, share, 2) + got
    else:
        summed = lax.psum(local_grad, "src")
        gradient = lax.dynamic_slice_in_dim(summed, own * share, share, 2)
    return (iterate, gradient)


def solution(mesh):
    placed = (
        P("gx", "gy", None),
        P(),
        P("src"),
        P("src", "gx", "gy", None),
        P("src", "gx", "gy", None),
    )
    return jax.shard_map(
        on_device,
        mesh=mesh,
        in_specs=placed,
        out_specs=(P("src", "gx", "gy", None), P("gx", "gy", "src")),
        check_vma=False,
    )
```

```python
import jax
import jax.numpy as jnp
from jax import lax
from jax.sharding import PartitionSpec as P
from jax.experimental import pallas as pl

ITERS = 2


INJECT = 4.0


def padded_2(block, sides, width):
    (axis_x, dim_x), (axis_y, dim_y) = sides
    pieces = {}
    for axis, dim in sides:
        count = lax.axis_size(axis)
        forward = [(i, i + 1) for i in range(count - 1)]
        backward = [(target, source) for source, target in forward]
        low = lax.ppermute(
            lax.slice_in_dim(block, block.shape[dim] - width, None, axis=dim), axis, forward
        )
        high = lax.ppermute(lax.slice_in_dim(block, 0, width, axis=dim), axis, backward)
        pieces[axis] = (low, high)
    low_x, high_x = pieces[axis_x]
    low_y, high_y = pieces[axis_y]
    middle = jnp.concatenate([low_x, block, high_x], axis=dim_x)
    rim = [(0, 0)] * block.ndim
    rim[dim_x] = (width, width)
    low_y = jnp.pad(low_y, rim)
    high_y = jnp.pad(high_y, rim)
    return jnp.concatenate([low_y, middle, high_y], axis=dim_y)


def allsum(value, axes):
    for axis in axes:
        count = lax.axis_size(axis)
        if count & (count - 1):
            value = lax.psum(value, axis)
            continue
        shift = 0
        if (count.bit_length() - 1) % 2:
            value = value + lax.ppermute(value, axis, [(i, i ^ 1) for i in range(count)])
            shift = 1
        while (1 << shift) < count:
            got = [
                lax.ppermute(value, axis, [(i, i ^ (d << shift)) for i in range(count)])
                for d in (1, 2, 3)
            ]
            value = (value + got[0]) + (got[1] + got[2])
            shift += 2
    return value


def conductances(sig_pad):
    full = jnp.pad(sig_pad, ((0, 0), (0, 0), (1, 1)))
    cond_x = 0.5 * (full[1:, 1:-1, 1:-1] + full[:-1, 1:-1, 1:-1])
    cond_y = 0.5 * (full[1:-1, 1:, 1:-1] + full[1:-1, :-1, 1:-1])
    cond_z = 0.5 * (full[1:-1, 1:-1, 1:] + full[1:-1, 1:-1, :-1])
    return (cond_x, cond_y, cond_z)


def operator(padded, conds):
    full = jnp.pad(padded, ((0, 0), (0, 0), (0, 0), (1, 1)))
    flux_x = conds[0] * (full[:, 1:, 1:-1, 1:-1] - full[:, :-1, 1:-1, 1:-1])
    flux_y = conds[1] * (full[:, 1:-1, 1:, 1:-1] - full[:, 1:-1, :-1, 1:-1])
    flux_z = conds[2] * (full[:, 1:-1, 1:-1, 1:] - full[:, 1:-1, 1:-1, :-1])
    return (
        flux_x[:, :-1]
        - flux_x[:, 1:]
        + (flux_y[:, :, :-1] - flux_y[:, :, 1:])
        + (flux_z[..., :-1] - flux_z[..., 1:])
    )


def gram_of(left, right):
    return jnp.einsum("axyz,bxyz->ab", left, right, precision=lax.Precision.HIGHEST)


def combine_cols(field, matrix):
    return jnp.einsum("axyz,ab->bxyz", field, matrix, precision=lax.Precision.HIGHEST)


def posdef_solve(matrix, right):
    lower = jnp.linalg.cholesky(matrix)
    middle = lax.linalg.triangular_solve(lower, right, left_side=True, lower=True)
    return lax.linalg.triangular_solve(lower, middle, left_side=True, lower=True, transpose_a=True)


def one_hot(cells, start, count):
    return (cells[:, None] == start + jnp.arange(count, dtype=jnp.int32)[None, :]).astype(
        jnp.float32
    )


def face_terms(field_pad, adjoint_pad):
    fu = jnp.pad(field_pad, ((0, 0), (0, 0), (0, 0), (1, 1)))
    fl = jnp.pad(adjoint_pad, ((0, 0), (0, 0), (0, 0), (1, 1)))
    term_x = jnp.sum(
        (fu[:, 1:, 1:-1, 1:-1] - fu[:, :-1, 1:-1, 1:-1])
        * (fl[:, 1:, 1:-1, 1:-1] - fl[:, :-1, 1:-1, 1:-1]),
        axis=0,
    )
    term_y = jnp.sum(
        (fu[:, 1:-1, 1:, 1:-1] - fu[:, 1:-1, :-1, 1:-1])
        * (fl[:, 1:-1, 1:, 1:-1] - fl[:, 1:-1, :-1, 1:-1]),
        axis=0,
    )
    term_z = jnp.sum(
        (fu[:, 1:-1, 1:-1, 1:] - fu[:, 1:-1, 1:-1, :-1])
        * (fl[:, 1:-1, 1:-1, 1:] - fl[:, 1:-1, 1:-1, :-1]),
        axis=0,
    )
    return (term_x, term_y, term_z)


HI = lax.Precision.HIGHEST

def _mm(a, b):
    return jnp.dot(a, b, precision=HI, preferred_element_type=jnp.float32)

def _tr(a):
    return jnp.transpose(a)

def _solve(matrix, right):
    n = matrix.shape[0]
    rows = lax.broadcasted_iota(jnp.int32, matrix.shape, 0)
    lanes = lax.broadcasted_iota(jnp.int32, matrix.shape, 1)
    lane_r = lax.broadcasted_iota(jnp.int32, (1, n), 1)

    def step(j, carry):
        m, r = carry
        pick = rows == j
        row_m = jnp.sum(jnp.where(pick, m, 0.0), axis=0, keepdims=True)
        row_r = jnp.sum(jnp.where(pick, r, 0.0), axis=0, keepdims=True)
        pivot = jnp.sum(jnp.where(lane_r == j, row_m, 0.0), axis=1, keepdims=True)
        col = jnp.sum(jnp.where(lanes == j, m, 0.0), axis=1, keepdims=True)
        row_m = row_m / pivot
        row_r = row_r / pivot
        m = jnp.where(pick, row_m, m - col * row_m)
        r = jnp.where(pick, row_r, r - col * row_r)
        return m, r

    _, out = lax.fori_loop(0, n, step, (matrix, right))
    return out

def steps_kernel(grams_ref, out_ref):
    g_rr = grams_ref[0]
    g_rq = grams_ref[1]
    g_qq = grams_ref[2]
    g_qw = grams_ref[3]
    n = g_rr.shape[0]
    step0 = _solve(g_rq, g_rr)
    cross = _mm(g_rq, step0)
    step0_t = _tr(step0)
    new_gram = g_rr - cross - _tr(cross) + _mm(step0_t, _mm(g_qq, step0))
    turn = _solve(g_rr, new_gram)
    eye = (lax.broadcasted_iota(jnp.int32, (n, n), 0) == lax.broadcasted_iota(jnp.int32, (n, n), 1)).astype(jnp.float32)
    keep = eye + turn
    keep_t = _tr(keep)
    curv = (_mm(keep_t, _mm(g_rq, keep)) - _mm(keep_t, _mm(g_qq, step0))
            - _mm(step0_t, _mm(g_qq, keep)) + _mm(step0_t, _mm(g_qw, step0)))
    step1 = _solve(curv, new_gram)
    out_ref[0] = step0
    out_ref[1] = turn
    out_ref[2] = step1

def steps(grams):
    n = grams.shape[1]
    return pl.pallas_call(steps_kernel, out_shape=jax.ShapeDtypeStruct((3, n, n), jnp.float32))(grams)


def on_device(conductivity, electrodes, pair_order, initial_fields, adjoint_fields):
    cells_x, cells_y, cells_z = conductivity.shape
    columns = initial_fields.shape[0]
    total_y = lax.axis_size("gy") * cells_y
    start_x = lax.axis_index("gx") * cells_x
    start_y = lax.axis_index("gy") * cells_y
    picked = jnp.take(electrodes, pair_order, axis=0)

    def point_source(flat):
        xs = flat // (total_y * cells_z)
        ys = flat // cells_z % total_y
        zs = flat % cells_z
        return jnp.einsum(
            "cx,cy,cz->cxyz",
            one_hot(xs, start_x, cells_x),
            one_hot(ys, start_y, cells_y),
            one_hot(zs, 0, cells_z),
        )

    right = INJECT * (point_source(picked[:, 0]) - point_source(picked[:, 1]))
    sides = (("gx", 1), ("gy", 2))
    grid_axes = ("gx", "gy")
    stacked = jnp.concatenate([conductivity[None], initial_fields, adjoint_fields], axis=0)
    padded = padded_2(stacked, sides, 1)
    conds = conductances(padded[0])
    iter_pad = padded[1 : 1 + columns]
    adjoint_pad = padded[1 + columns :]
    residual = right - operator(iter_pad, conds)
    res_pad = padded_2(residual, sides, 1)
    image = operator(res_pad, conds)
    image_pad = padded_2(image, sides, 1)
    image2 = operator(image_pad, conds)
    grams = allsum(
        jnp.stack(
            [
                gram_of(residual, residual),
                gram_of(residual, image),
                gram_of(image, image),
                gram_of(image, image2),
            ]
        ),
        grid_axes,
    )

    solved = steps(grams)
    step0, turn, step1 = solved[0], solved[1], solved[2]
    res1_pad = res_pad - combine_cols(image_pad, step0)
    dir1_pad = res1_pad + combine_cols(res_pad, turn)
    it1_pad = iter_pad + combine_cols(res_pad, step0)
    it2_pad = it1_pad + combine_cols(dir1_pad, step1)
    iterate = it2_pad[:, 1:-1, 1:-1]
    term_x, term_y, term_z = face_terms(it2_pad, adjoint_pad)
    local_grad = (
        -0.5
        / columns
        * (
            term_x[:-1]
            + term_x[1:]
            + term_y[:, :-1]
            + term_y[:, 1:]
            + term_z[..., :-1]
            + term_z[..., 1:]
        )
    )
    groups = lax.axis_size("src")
    share = cells_z // groups
    own = lax.axis_index("src")
    if groups == 2:
        other = 1 - own
        sent = lax.dynamic_slice_in_dim(local_grad, other * share, share, 2)
        got = lax.ppermute(sent, "src", [(0, 1), (1, 0)])
        gradient = lax.dynamic_slice_in_dim(local_grad, own * share, share, 2) + got
    else:
        summed = lax.psum(local_grad, "src")
        gradient = lax.dynamic_slice_in_dim(summed, own * share, share, 2)
    return (iterate, gradient)


def solution(mesh):
    placed = (
        P("gx", "gy", None),
        P(),
        P("src"),
        P("src", "gx", "gy", None),
        P("src", "gx", "gy", None),
    )
    return jax.shard_map(
        on_device,
        mesh=mesh,
        in_specs=placed,
        out_specs=(P("src", "gx", "gy", None), P("gx", "gy", "src")),
        check_vma=False,
    )
```

```python
import jax
import jax.numpy as jnp
from jax import lax
from jax.sharding import PartitionSpec as P
from jax.experimental import pallas as pl

ITERS = 2


INJECT = 4.0


def padded_2(block, sides, width):
    (axis_x, dim_x), (axis_y, dim_y) = sides
    pieces = {}
    for axis, dim in sides:
        count = lax.axis_size(axis)
        forward = [(i, i + 1) for i in range(count - 1)]
        backward = [(target, source) for source, target in forward]
        low = lax.ppermute(
            lax.slice_in_dim(block, block.shape[dim] - width, None, axis=dim), axis, forward
        )
        high = lax.ppermute(lax.slice_in_dim(block, 0, width, axis=dim), axis, backward)
        pieces[axis] = (low, high)
    low_x, high_x = pieces[axis_x]
    low_y, high_y = pieces[axis_y]
    middle = jnp.concatenate([low_x, block, high_x], axis=dim_x)
    rim = [(0, 0)] * block.ndim
    rim[dim_x] = (width, width)
    low_y = jnp.pad(low_y, rim)
    high_y = jnp.pad(high_y, rim)
    return jnp.concatenate([low_y, middle, high_y], axis=dim_y)


def allsum(value, axes):
    for axis in axes:
        count = lax.axis_size(axis)
        if count & (count - 1):
            value = lax.psum(value, axis)
            continue
        shift = 0
        if (count.bit_length() - 1) % 2:
            value = value + lax.ppermute(value, axis, [(i, i ^ 1) for i in range(count)])
            shift = 1
        while (1 << shift) < count:
            got = [
                lax.ppermute(value, axis, [(i, i ^ (d << shift)) for i in range(count)])
                for d in (1, 2, 3)
            ]
            value = (value + got[0]) + (got[1] + got[2])
            shift += 2
    return value


def conductances(sig_pad):
    full = jnp.pad(sig_pad, ((0, 0), (0, 0), (1, 1)))
    cond_x = 0.5 * (full[1:, 1:-1, 1:-1] + full[:-1, 1:-1, 1:-1])
    cond_y = 0.5 * (full[1:-1, 1:, 1:-1] + full[1:-1, :-1, 1:-1])
    cond_z = 0.5 * (full[1:-1, 1:-1, 1:] + full[1:-1, 1:-1, :-1])
    return (cond_x, cond_y, cond_z)


def operator(padded, conds):
    full = jnp.pad(padded, ((0, 0), (0, 0), (0, 0), (1, 1)))
    flux_x = conds[0] * (full[:, 1:, 1:-1, 1:-1] - full[:, :-1, 1:-1, 1:-1])
    flux_y = conds[1] * (full[:, 1:-1, 1:, 1:-1] - full[:, 1:-1, :-1, 1:-1])
    flux_z = conds[2] * (full[:, 1:-1, 1:-1, 1:] - full[:, 1:-1, 1:-1, :-1])
    return (
        flux_x[:, :-1]
        - flux_x[:, 1:]
        + (flux_y[:, :, :-1] - flux_y[:, :, 1:])
        + (flux_z[..., :-1] - flux_z[..., 1:])
    )


def gram_of(left, right):
    return jnp.einsum("axyz,bxyz->ab", left, right, precision=lax.Precision.HIGHEST)


def combine_cols(field, matrix):
    return jnp.einsum("axyz,ab->bxyz", field, matrix, precision=lax.Precision.HIGHEST)


def posdef_solve(matrix, right):
    lower = jnp.linalg.cholesky(matrix)
    middle = lax.linalg.triangular_solve(lower, right, left_side=True, lower=True)
    return lax.linalg.triangular_solve(lower, middle, left_side=True, lower=True, transpose_a=True)


def one_hot(cells, start, count):
    return (cells[:, None] == start + jnp.arange(count, dtype=jnp.int32)[None, :]).astype(
        jnp.float32
    )


def face_terms(field_pad, adjoint_pad):
    fu = jnp.pad(field_pad, ((0, 0), (0, 0), (0, 0), (1, 1)))
    fl = jnp.pad(adjoint_pad, ((0, 0), (0, 0), (0, 0), (1, 1)))
    term_x = jnp.sum(
        (fu[:, 1:, 1:-1, 1:-1] - fu[:, :-1, 1:-1, 1:-1])
        * (fl[:, 1:, 1:-1, 1:-1] - fl[:, :-1, 1:-1, 1:-1]),
        axis=0,
    )
    term_y = jnp.sum(
        (fu[:, 1:-1, 1:, 1:-1] - fu[:, 1:-1, :-1, 1:-1])
        * (fl[:, 1:-1, 1:, 1:-1] - fl[:, 1:-1, :-1, 1:-1]),
        axis=0,
    )
    term_z = jnp.sum(
        (fu[:, 1:-1, 1:-1, 1:] - fu[:, 1:-1, 1:-1, :-1])
        * (fl[:, 1:-1, 1:-1, 1:] - fl[:, 1:-1, 1:-1, :-1]),
        axis=0,
    )
    return (term_x, term_y, term_z)


HI = lax.Precision.HIGHEST

def _mm(a, b):
    return jnp.dot(a, b, precision=HI, preferred_element_type=jnp.float32)

def _tr(a):
    return jnp.transpose(a)

def _solve(pairs, unroll):
    n = pairs[0][0].shape[0]
    shape = pairs[0][0].shape
    rows = lax.broadcasted_iota(jnp.int32, shape, 0)
    lanes = lax.broadcasted_iota(jnp.int32, shape, 1)
    lane_r = lax.broadcasted_iota(jnp.int32, (1, n), 1)

    def step(j, carry):
        pick = rows == j
        out = []
        for m, r in carry:
            row_m = jnp.sum(jnp.where(pick, m, 0.0), axis=0, keepdims=True)
            row_r = jnp.sum(jnp.where(pick, r, 0.0), axis=0, keepdims=True)
            pivot = jnp.sum(jnp.where(lane_r == j, row_m, 0.0), axis=1, keepdims=True)
            col = jnp.sum(jnp.where(lanes == j, m, 0.0), axis=1, keepdims=True)
            row_m = row_m / pivot
            row_r = row_r / pivot
            m = jnp.where(pick, row_m, m - col * row_m)
            r = jnp.where(pick, row_r, r - col * row_r)
            out.append((m, r))
        return tuple(out)

    done = lax.fori_loop(0, n, step, tuple(pairs), unroll=unroll)
    return [r for _, r in done]


def steps_kernel(grams_ref, out_ref):
    g_rr = grams_ref[0]
    g_rq = grams_ref[1]
    g_qq = grams_ref[2]
    g_qw = grams_ref[3]
    n = g_rr.shape[0]
    eye = (
        lax.broadcasted_iota(jnp.int32, (n, n), 0) == lax.broadcasted_iota(jnp.int32, (n, n), 1)
    ).astype(jnp.float32)
    step0, rr_inv = _solve([(g_rq, g_rr), (g_rr, eye)], 2)
    cross = _mm(g_rq, step0)
    step0_t = _tr(step0)
    new_gram = g_rr - cross - _tr(cross) + _mm(step0_t, _mm(g_qq, step0))
    turn = _mm(rr_inv, new_gram)
    keep = eye + turn
    keep_t = _tr(keep)
    curv = (
        _mm(keep_t, _mm(g_rq, keep))
        - _mm(keep_t, _mm(g_qq, step0))
        - _mm(step0_t, _mm(g_qq, keep))
        + _mm(step0_t, _mm(g_qw, step0))
    )
    (step1,) = _solve([(curv, new_gram)], 4)
    out_ref[0] = step0
    out_ref[1] = turn
    out_ref[2] = step1


def steps(grams):
    n = grams.shape[1]
    return pl.pallas_call(steps_kernel, out_shape=jax.ShapeDtypeStruct((3, n, n), jnp.float32))(grams)


def on_device(conductivity, electrodes, pair_order, initial_fields, adjoint_fields):
    cells_x, cells_y, cells_z = conductivity.shape
    columns = initial_fields.shape[0]
    total_y = lax.axis_size("gy") * cells_y
    start_x = lax.axis_index("gx") * cells_x
    start_y = lax.axis_index("gy") * cells_y
    picked = jnp.take(electrodes, pair_order, axis=0)

    def point_source(flat):
        xs = flat // (total_y * cells_z)
        ys = flat // cells_z % total_y
        zs = flat % cells_z
        return jnp.einsum(
            "cx,cy,cz->cxyz",
            one_hot(xs, start_x, cells_x),
            one_hot(ys, start_y, cells_y),
            one_hot(zs, 0, cells_z),
        )

    right = INJECT * (point_source(picked[:, 0]) - point_source(picked[:, 1]))
    sides = (("gx", 1), ("gy", 2))
    grid_axes = ("gx", "gy")
    stacked = jnp.concatenate([conductivity[None], initial_fields, adjoint_fields], axis=0)
    padded = padded_2(stacked, sides, 1)
    conds = conductances(padded[0])
    iter_pad = padded[1 : 1 + columns]
    adjoint_pad = padded[1 + columns :]
    residual = right - operator(iter_pad, conds)
    res_pad = padded_2(residual, sides, 1)
    image = operator(res_pad, conds)
    image_pad = padded_2(image, sides, 1)
    image2 = operator(image_pad, conds)
    grams = allsum(
        jnp.stack(
            [
                gram_of(residual, residual),
                gram_of(residual, image),
                gram_of(image, image),
                gram_of(image, image2),
            ]
        ),
        grid_axes,
    )

    solved = steps(grams)
    step0, turn, step1 = solved[0], solved[1], solved[2]
    res1_pad = res_pad - combine_cols(image_pad, step0)
    dir1_pad = res1_pad + combine_cols(res_pad, turn)
    it1_pad = iter_pad + combine_cols(res_pad, step0)
    it2_pad = it1_pad + combine_cols(dir1_pad, step1)
    iterate = it2_pad[:, 1:-1, 1:-1]
    term_x, term_y, term_z = face_terms(it2_pad, adjoint_pad)
    local_grad = (
        -0.5
        / columns
        * (
            term_x[:-1]
            + term_x[1:]
            + term_y[:, :-1]
            + term_y[:, 1:]
            + term_z[..., :-1]
            + term_z[..., 1:]
        )
    )
    groups = lax.axis_size("src")
    share = cells_z // groups
    own = lax.axis_index("src")
    if groups == 2:
        other = 1 - own
        sent = lax.dynamic_slice_in_dim(local_grad, other * share, share, 2)
        got = lax.ppermute(sent, "src", [(0, 1), (1, 0)])
        gradient = lax.dynamic_slice_in_dim(local_grad, own * share, share, 2) + got
    else:
        summed = lax.psum(local_grad, "src")
        gradient = lax.dynamic_slice_in_dim(summed, own * share, share, 2)
    return (iterate, gradient)


def solution(mesh):
    placed = (
        P("gx", "gy", None),
        P(),
        P("src"),
        P("src", "gx", "gy", None),
        P("src", "gx", "gy", None),
    )
    return jax.shard_map(
        on_device,
        mesh=mesh,
        in_specs=placed,
        out_specs=(P("src", "gx", "gy", None), P("gx", "gy", "src")),
        check_vma=False,
    )
```

```python
import jax
import jax.numpy as jnp
from jax import lax
from jax.sharding import PartitionSpec as P
from jax.experimental import pallas as pl

ITERS = 2


INJECT = 4.0


def padded_2(block, sides, width):
    (axis_x, dim_x), (axis_y, dim_y) = sides
    pieces = {}
    for axis, dim in sides:
        count = lax.axis_size(axis)
        place = lax.axis_index(axis)
        forward = [(i, (i + 1) % count) for i in range(count)]
        backward = [(target, source) for source, target in forward]
        low = lax.ppermute(
            lax.slice_in_dim(block, block.shape[dim] - width, None, axis=dim), axis, forward
        )
        high = lax.ppermute(lax.slice_in_dim(block, 0, width, axis=dim), axis, backward)
        low = jnp.where(place == 0, jnp.zeros_like(low), low)
        high = jnp.where(place == count - 1, jnp.zeros_like(high), high)
        pieces[axis] = (low, high)
    low_x, high_x = pieces[axis_x]
    low_y, high_y = pieces[axis_y]
    middle = jnp.concatenate([low_x, block, high_x], axis=dim_x)
    rim = [(0, 0)] * block.ndim
    rim[dim_x] = (width, width)
    low_y = jnp.pad(low_y, rim)
    high_y = jnp.pad(high_y, rim)
    return jnp.concatenate([low_y, middle, high_y], axis=dim_y)


def allsum(value, axes):
    for axis in axes:
        count = lax.axis_size(axis)
        if count & (count - 1):
            value = lax.psum(value, axis)
            continue
        shift = 0
        if (count.bit_length() - 1) % 2:
            value = value + lax.ppermute(value, axis, [(i, i ^ 1) for i in range(count)])
            shift = 1
        while (1 << shift) < count:
            got = [
                lax.ppermute(value, axis, [(i, i ^ (d << shift)) for i in range(count)])
                for d in (1, 2, 3)
            ]
            value = (value + got[0]) + (got[1] + got[2])
            shift += 2
    return value


def conductances(sig_pad):
    full = jnp.pad(sig_pad, ((0, 0), (0, 0), (1, 1)))
    cond_x = 0.5 * (full[1:, 1:-1, 1:-1] + full[:-1, 1:-1, 1:-1])
    cond_y = 0.5 * (full[1:-1, 1:, 1:-1] + full[1:-1, :-1, 1:-1])
    cond_z = 0.5 * (full[1:-1, 1:-1, 1:] + full[1:-1, 1:-1, :-1])
    return (cond_x, cond_y, cond_z)


def operator(padded, conds):
    full = jnp.pad(padded, ((0, 0), (0, 0), (0, 0), (1, 1)))
    flux_x = conds[0] * (full[:, 1:, 1:-1, 1:-1] - full[:, :-1, 1:-1, 1:-1])
    flux_y = conds[1] * (full[:, 1:-1, 1:, 1:-1] - full[:, 1:-1, :-1, 1:-1])
    flux_z = conds[2] * (full[:, 1:-1, 1:-1, 1:] - full[:, 1:-1, 1:-1, :-1])
    return (
        flux_x[:, :-1]
        - flux_x[:, 1:]
        + (flux_y[:, :, :-1] - flux_y[:, :, 1:])
        + (flux_z[..., :-1] - flux_z[..., 1:])
    )


def gram_of(left, right):
    return jnp.einsum("axyz,bxyz->ab", left, right, precision=lax.Precision.HIGHEST)


def combine_cols(field, matrix):
    return jnp.einsum("axyz,ab->bxyz", field, matrix, precision=lax.Precision.HIGHEST)


def posdef_solve(matrix, right):
    lower = jnp.linalg.cholesky(matrix)
    middle = lax.linalg.triangular_solve(lower, right, left_side=True, lower=True)
    return lax.linalg.triangular_solve(lower, middle, left_side=True, lower=True, transpose_a=True)


def one_hot(cells, start, count):
    return (cells[:, None] == start + jnp.arange(count, dtype=jnp.int32)[None, :]).astype(
        jnp.float32
    )


def face_terms(field_pad, adjoint_pad):
    fu = jnp.pad(field_pad, ((0, 0), (0, 0), (0, 0), (1, 1)))
    fl = jnp.pad(adjoint_pad, ((0, 0), (0, 0), (0, 0), (1, 1)))
    term_x = jnp.sum(
        (fu[:, 1:, 1:-1, 1:-1] - fu[:, :-1, 1:-1, 1:-1])
        * (fl[:, 1:, 1:-1, 1:-1] - fl[:, :-1, 1:-1, 1:-1]),
        axis=0,
    )
    term_y = jnp.sum(
        (fu[:, 1:-1, 1:, 1:-1] - fu[:, 1:-1, :-1, 1:-1])
        * (fl[:, 1:-1, 1:, 1:-1] - fl[:, 1:-1, :-1, 1:-1]),
        axis=0,
    )
    term_z = jnp.sum(
        (fu[:, 1:-1, 1:-1, 1:] - fu[:, 1:-1, 1:-1, :-1])
        * (fl[:, 1:-1, 1:-1, 1:] - fl[:, 1:-1, 1:-1, :-1]),
        axis=0,
    )
    return (term_x, term_y, term_z)


HI = lax.Precision.HIGHEST

def _mm(a, b):
    return jnp.dot(a, b, precision=HI, preferred_element_type=jnp.float32)

def _tr(a):
    return jnp.transpose(a)

def _solve(pairs, unroll):
    n = pairs[0][0].shape[0]
    shape = pairs[0][0].shape
    rows = lax.broadcasted_iota(jnp.int32, shape, 0)
    lanes = lax.broadcasted_iota(jnp.int32, shape, 1)
    lane_r = lax.broadcasted_iota(jnp.int32, (1, n), 1)

    def step(j, carry):
        pick = rows == j
        out = []
        for m, r in carry:
            row_m = jnp.sum(jnp.where(pick, m, 0.0), axis=0, keepdims=True)
            row_r = jnp.sum(jnp.where(pick, r, 0.0), axis=0, keepdims=True)
            pivot = jnp.sum(jnp.where(lane_r == j, row_m, 0.0), axis=1, keepdims=True)
            col = jnp.sum(jnp.where(lanes == j, m, 0.0), axis=1, keepdims=True)
            row_m = row_m / pivot
            row_r = row_r / pivot
            m = jnp.where(pick, row_m, m - col * row_m)
            r = jnp.where(pick, row_r, r - col * row_r)
            out.append((m, r))
        return tuple(out)

    done = lax.fori_loop(0, n, step, tuple(pairs), unroll=unroll)
    return [r for _, r in done]


def steps_kernel(grams_ref, out_ref):
    g_rr = grams_ref[0]
    g_rq = grams_ref[1]
    g_qq = grams_ref[2]
    g_qw = grams_ref[3]
    n = g_rr.shape[0]
    eye = (
        lax.broadcasted_iota(jnp.int32, (n, n), 0) == lax.broadcasted_iota(jnp.int32, (n, n), 1)
    ).astype(jnp.float32)
    step0, rr_inv = _solve([(g_rq, g_rr), (g_rr, eye)], 2)
    cross = _mm(g_rq, step0)
    step0_t = _tr(step0)
    new_gram = g_rr - cross - _tr(cross) + _mm(step0_t, _mm(g_qq, step0))
    turn = _mm(rr_inv, new_gram)
    keep = eye + turn
    keep_t = _tr(keep)
    curv = (
        _mm(keep_t, _mm(g_rq, keep))
        - _mm(keep_t, _mm(g_qq, step0))
        - _mm(step0_t, _mm(g_qq, keep))
        + _mm(step0_t, _mm(g_qw, step0))
    )
    (step1,) = _solve([(curv, new_gram)], 4)
    out_ref[0] = step0
    out_ref[1] = turn
    out_ref[2] = step1


def steps(grams):
    n = grams.shape[1]
    return pl.pallas_call(steps_kernel, out_shape=jax.ShapeDtypeStruct((3, n, n), jnp.float32))(grams)


def on_device(conductivity, electrodes, pair_order, initial_fields, adjoint_fields):
    cells_x, cells_y, cells_z = conductivity.shape
    columns = initial_fields.shape[0]
    total_y = lax.axis_size("gy") * cells_y
    start_x = lax.axis_index("gx") * cells_x
    start_y = lax.axis_index("gy") * cells_y
    picked = jnp.take(electrodes, pair_order, axis=0)

    def point_source(flat):
        xs = flat // (total_y * cells_z)
        ys = flat // cells_z % total_y
        zs = flat % cells_z
        return jnp.einsum(
            "cx,cy,cz->cxyz",
            one_hot(xs, start_x, cells_x),
            one_hot(ys, start_y, cells_y),
            one_hot(zs, 0, cells_z),
        )

    right = INJECT * (point_source(picked[:, 0]) - point_source(picked[:, 1]))
    sides = (("gx", 1), ("gy", 2))
    grid_axes = ("gx", "gy")
    stacked = jnp.concatenate([conductivity[None], initial_fields, adjoint_fields], axis=0)
    padded = padded_2(stacked, sides, 1)
    conds = conductances(padded[0])
    iter_pad = padded[1 : 1 + columns]
    adjoint_pad = padded[1 + columns :]
    residual = right - operator(iter_pad, conds)
    res_pad = padded_2(residual, sides, 1)
    image = operator(res_pad, conds)
    image_pad = padded_2(image, sides, 1)
    image2 = operator(image_pad, conds)
    grams = allsum(
        jnp.stack(
            [
                gram_of(residual, residual),
                gram_of(residual, image),
                gram_of(image, image),
                gram_of(image, image2),
            ]
        ),
        grid_axes,
    )

    solved = steps(grams)
    step0, turn, step1 = solved[0], solved[1], solved[2]
    res1_pad = res_pad - combine_cols(image_pad, step0)
    dir1_pad = res1_pad + combine_cols(res_pad, turn)
    it1_pad = iter_pad + combine_cols(res_pad, step0)
    it2_pad = it1_pad + combine_cols(dir1_pad, step1)
    iterate = it2_pad[:, 1:-1, 1:-1]
    term_x, term_y, term_z = face_terms(it2_pad, adjoint_pad)
    local_grad = (
        -0.5
        / columns
        * (
            term_x[:-1]
            + term_x[1:]
            + term_y[:, :-1]
            + term_y[:, 1:]
            + term_z[..., :-1]
            + term_z[..., 1:]
        )
    )
    groups = lax.axis_size("src")
    share = cells_z // groups
    own = lax.axis_index("src")
    if groups == 2:
        other = 1 - own
        sent = lax.dynamic_slice_in_dim(local_grad, other * share, share, 2)
        got = lax.ppermute(sent, "src", [(0, 1), (1, 0)])
        gradient = lax.dynamic_slice_in_dim(local_grad, own * share, share, 2) + got
    else:
        summed = lax.psum(local_grad, "src")
        gradient = lax.dynamic_slice_in_dim(summed, own * share, share, 2)
    return (iterate, gradient)


def solution(mesh):
    placed = (
        P("gx", "gy", None),
        P(),
        P("src"),
        P("src", "gx", "gy", None),
        P("src", "gx", "gy", None),
    )
    return jax.shard_map(
        on_device,
        mesh=mesh,
        in_specs=placed,
        out_specs=(P("src", "gx", "gy", None), P("gx", "gy", "src")),
        check_vma=False,
    )
```

```python
import jax
import jax.numpy as jnp
from jax import lax
from jax.sharding import PartitionSpec as P
from jax.experimental import pallas as pl

ITERS = 2


INJECT = 4.0


def padded_2(block, sides, width):
    (axis_x, dim_x), (axis_y, dim_y) = sides
    pieces = {}
    for axis, dim in sides:
        count = lax.axis_size(axis)
        place = lax.axis_index(axis)
        forward = [(i, (i + 1) % count) for i in range(count)]
        backward = [(target, source) for source, target in forward]
        top = lax.slice_in_dim(block, block.shape[dim] - width, None, axis=dim)
        bottom = lax.slice_in_dim(block, 0, width, axis=dim)
        top = jnp.where(place == count - 1, jnp.zeros_like(top), top)
        bottom = jnp.where(place == 0, jnp.zeros_like(bottom), bottom)
        low = lax.ppermute(top, axis, forward)
        high = lax.ppermute(bottom, axis, backward)
        pieces[axis] = (low, high)
    low_x, high_x = pieces[axis_x]
    low_y, high_y = pieces[axis_y]
    middle = jnp.concatenate([low_x, block, high_x], axis=dim_x)
    rim = [(0, 0)] * block.ndim
    rim[dim_x] = (width, width)
    low_y = jnp.pad(low_y, rim)
    high_y = jnp.pad(high_y, rim)
    return jnp.concatenate([low_y, middle, high_y], axis=dim_y)


def allsum(value, axes):
    for axis in axes:
        count = lax.axis_size(axis)
        if count & (count - 1):
            value = lax.psum(value, axis)
            continue
        shift = 0
        if (count.bit_length() - 1) % 2:
            value = value + lax.ppermute(value, axis, [(i, i ^ 1) for i in range(count)])
            shift = 1
        while (1 << shift) < count:
            got = [
                lax.ppermute(value, axis, [(i, i ^ (d << shift)) for i in range(count)])
                for d in (1, 2, 3)
            ]
            value = (value + got[0]) + (got[1] + got[2])
            shift += 2
    return value


def conductances(sig_pad):
    full = jnp.pad(sig_pad, ((0, 0), (0, 0), (1, 1)))
    cond_x = 0.5 * (full[1:, 1:-1, 1:-1] + full[:-1, 1:-1, 1:-1])
    cond_y = 0.5 * (full[1:-1, 1:, 1:-1] + full[1:-1, :-1, 1:-1])
    cond_z = 0.5 * (full[1:-1, 1:-1, 1:] + full[1:-1, 1:-1, :-1])
    return (cond_x, cond_y, cond_z)


def operator(padded, conds):
    full = jnp.pad(padded, ((0, 0), (0, 0), (0, 0), (1, 1)))
    flux_x = conds[0] * (full[:, 1:, 1:-1, 1:-1] - full[:, :-1, 1:-1, 1:-1])
    flux_y = conds[1] * (full[:, 1:-1, 1:, 1:-1] - full[:, 1:-1, :-1, 1:-1])
    flux_z = conds[2] * (full[:, 1:-1, 1:-1, 1:] - full[:, 1:-1, 1:-1, :-1])
    return (
        flux_x[:, :-1]
        - flux_x[:, 1:]
        + (flux_y[:, :, :-1] - flux_y[:, :, 1:])
        + (flux_z[..., :-1] - flux_z[..., 1:])
    )


def gram_of(left, right):
    return jnp.einsum("axyz,bxyz->ab", left, right, precision=lax.Precision.HIGHEST)


def combine_cols(field, matrix):
    return jnp.einsum("axyz,ab->bxyz", field, matrix, precision=lax.Precision.HIGHEST)


def posdef_solve(matrix, right):
    lower = jnp.linalg.cholesky(matrix)
    middle = lax.linalg.triangular_solve(lower, right, left_side=True, lower=True)
    return lax.linalg.triangular_solve(lower, middle, left_side=True, lower=True, transpose_a=True)


def one_hot(cells, start, count):
    return (cells[:, None] == start + jnp.arange(count, dtype=jnp.int32)[None, :]).astype(
        jnp.float32
    )


def face_terms(field_pad, adjoint_pad):
    fu = jnp.pad(field_pad, ((0, 0), (0, 0), (0, 0), (1, 1)))
    fl = jnp.pad(adjoint_pad, ((0, 0), (0, 0), (0, 0), (1, 1)))
    term_x = jnp.sum(
        (fu[:, 1:, 1:-1, 1:-1] - fu[:, :-1, 1:-1, 1:-1])
        * (fl[:, 1:, 1:-1, 1:-1] - fl[:, :-1, 1:-1, 1:-1]),
        axis=0,
    )
    term_y = jnp.sum(
        (fu[:, 1:-1, 1:, 1:-1] - fu[:, 1:-1, :-1, 1:-1])
        * (fl[:, 1:-1, 1:, 1:-1] - fl[:, 1:-1, :-1, 1:-1]),
        axis=0,
    )
    term_z = jnp.sum(
        (fu[:, 1:-1, 1:-1, 1:] - fu[:, 1:-1, 1:-1, :-1])
        * (fl[:, 1:-1, 1:-1, 1:] - fl[:, 1:-1, 1:-1, :-1]),
        axis=0,
    )
    return (term_x, term_y, term_z)


HI = lax.Precision.HIGHEST

def _mm(a, b):
    return jnp.dot(a, b, precision=HI, preferred_element_type=jnp.float32)

def _tr(a):
    return jnp.transpose(a)

def _solve(pairs, unroll):
    n = pairs[0][0].shape[0]
    shape = pairs[0][0].shape
    rows = lax.broadcasted_iota(jnp.int32, shape, 0)
    lanes = lax.broadcasted_iota(jnp.int32, shape, 1)
    lane_r = lax.broadcasted_iota(jnp.int32, (1, n), 1)

    def step(j, carry):
        pick = rows == j
        out = []
        for m, r in carry:
            row_m = jnp.sum(jnp.where(pick, m, 0.0), axis=0, keepdims=True)
            row_r = jnp.sum(jnp.where(pick, r, 0.0), axis=0, keepdims=True)
            pivot = jnp.sum(jnp.where(lane_r == j, row_m, 0.0), axis=1, keepdims=True)
            col = jnp.sum(jnp.where(lanes == j, m, 0.0), axis=1, keepdims=True)
            row_m = row_m / pivot
            row_r = row_r / pivot
            m = jnp.where(pick, row_m, m - col * row_m)
            r = jnp.where(pick, row_r, r - col * row_r)
            out.append((m, r))
        return tuple(out)

    done = lax.fori_loop(0, n, step, tuple(pairs), unroll=unroll)
    return [r for _, r in done]


def steps_kernel(grams_ref, out_ref):
    g_rr = grams_ref[0]
    g_rq = grams_ref[1]
    g_qq = grams_ref[2]
    g_qw = grams_ref[3]
    n = g_rr.shape[0]
    eye = (
        lax.broadcasted_iota(jnp.int32, (n, n), 0) == lax.broadcasted_iota(jnp.int32, (n, n), 1)
    ).astype(jnp.float32)
    step0, rr_inv = _solve([(g_rq, g_rr), (g_rr, eye)], 2)
    cross = _mm(g_rq, step0)
    step0_t = _tr(step0)
    new_gram = g_rr - cross - _tr(cross) + _mm(step0_t, _mm(g_qq, step0))
    turn = _mm(rr_inv, new_gram)
    keep = eye + turn
    keep_t = _tr(keep)
    curv = (
        _mm(keep_t, _mm(g_rq, keep))
        - _mm(keep_t, _mm(g_qq, step0))
        - _mm(step0_t, _mm(g_qq, keep))
        + _mm(step0_t, _mm(g_qw, step0))
    )
    (step1,) = _solve([(curv, new_gram)], 4)
    out_ref[0] = step0 + _mm(keep, step1)
    out_ref[1] = -_mm(step0, step1)


def steps(grams):
    n = grams.shape[1]
    return pl.pallas_call(steps_kernel, out_shape=jax.ShapeDtypeStruct((2, n, n), jnp.float32))(grams)


def on_device(conductivity, electrodes, pair_order, initial_fields, adjoint_fields):
    cells_x, cells_y, cells_z = conductivity.shape
    columns = initial_fields.shape[0]
    total_y = lax.axis_size("gy") * cells_y
    start_x = lax.axis_index("gx") * cells_x
    start_y = lax.axis_index("gy") * cells_y
    picked = jnp.take(electrodes, pair_order, axis=0)

    def point_source(flat):
        xs = flat // (total_y * cells_z)
        ys = flat // cells_z % total_y
        zs = flat % cells_z
        return jnp.einsum(
            "cx,cy,cz->cxyz",
            one_hot(xs, start_x, cells_x),
            one_hot(ys, start_y, cells_y),
            one_hot(zs, 0, cells_z),
        )

    right = INJECT * (point_source(picked[:, 0]) - point_source(picked[:, 1]))
    sides = (("gx", 1), ("gy", 2))
    grid_axes = ("gx", "gy")
    stacked = jnp.concatenate([conductivity[None], initial_fields, adjoint_fields], axis=0)
    padded = padded_2(stacked, sides, 1)
    conds = conductances(padded[0])
    iter_pad = padded[1 : 1 + columns]
    adjoint_pad = padded[1 + columns :]
    residual = right - operator(iter_pad, conds)
    res_pad = padded_2(residual, sides, 1)
    image = operator(res_pad, conds)
    image_pad = padded_2(image, sides, 1)
    image2 = operator(image_pad, conds)
    grams = allsum(
        jnp.stack(
            [
                gram_of(residual, residual),
                gram_of(residual, image),
                gram_of(image, image),
                gram_of(image, image2),
            ]
        ),
        grid_axes,
    )

    solved = steps(grams)
    it2_pad = iter_pad + combine_cols(res_pad, solved[0]) + combine_cols(image_pad, solved[1])
    iterate = it2_pad[:, 1:-1, 1:-1]
    term_x, term_y, term_z = face_terms(it2_pad, adjoint_pad)
    local_grad = (
        -0.5
        / columns
        * (
            term_x[:-1]
            + term_x[1:]
            + term_y[:, :-1]
            + term_y[:, 1:]
            + term_z[..., :-1]
            + term_z[..., 1:]
        )
    )
    groups = lax.axis_size("src")
    share = cells_z // groups
    own = lax.axis_index("src")
    if groups == 2:
        other = 1 - own
        sent = lax.dynamic_slice_in_dim(local_grad, other * share, share, 2)
        got = lax.ppermute(sent, "src", [(0, 1), (1, 0)])
        gradient = lax.dynamic_slice_in_dim(local_grad, own * share, share, 2) + got
    else:
        summed = lax.psum(local_grad, "src")
        gradient = lax.dynamic_slice_in_dim(summed, own * share, share, 2)
    return (iterate, gradient)


def solution(mesh):
    placed = (
        P("gx", "gy", None),
        P(),
        P("src"),
        P("src", "gx", "gy", None),
        P("src", "gx", "gy", None),
    )
    return jax.shard_map(
        on_device,
        mesh=mesh,
        in_specs=placed,
        out_specs=(P("src", "gx", "gy", None), P("gx", "gy", "src")),
        check_vma=False,
    )
```

```python
import jax
import jax.numpy as jnp
from jax import lax
from jax.sharding import PartitionSpec as P
from jax.experimental import pallas as pl

ITERS = 2


INJECT = 4.0


def padded_2(block, sides, width):
    (axis_x, dim_x), (axis_y, dim_y) = sides
    pieces = {}
    for axis, dim in sides:
        count = lax.axis_size(axis)
        place = lax.axis_index(axis)
        forward = [(i, (i + 1) % count) for i in range(count)]
        backward = [(target, source) for source, target in forward]
        top = lax.slice_in_dim(block, block.shape[dim] - width, None, axis=dim)
        bottom = lax.slice_in_dim(block, 0, width, axis=dim)
        top = jnp.where(place == count - 1, jnp.zeros_like(top), top)
        bottom = jnp.where(place == 0, jnp.zeros_like(bottom), bottom)
        low = lax.ppermute(top, axis, forward)
        high = lax.ppermute(bottom, axis, backward)
        pieces[axis] = (low, high)
    low_x, high_x = pieces[axis_x]
    low_y, high_y = pieces[axis_y]
    middle = jnp.concatenate([low_x, block, high_x], axis=dim_x)
    rim = [(0, 0)] * block.ndim
    rim[dim_x] = (width, width)
    low_y = jnp.pad(low_y, rim)
    high_y = jnp.pad(high_y, rim)
    return jnp.concatenate([low_y, middle, high_y], axis=dim_y)


def allsum(value, axes):
    for axis in axes:
        count = lax.axis_size(axis)
        if count & (count - 1):
            value = lax.psum(value, axis)
            continue
        shift = 0
        if (count.bit_length() - 1) % 2:
            value = value + lax.ppermute(value, axis, [(i, i ^ 1) for i in range(count)])
            shift = 1
        while (1 << shift) < count:
            got = [
                lax.ppermute(value, axis, [(i, i ^ (d << shift)) for i in range(count)])
                for d in (1, 2, 3)
            ]
            value = (value + got[0]) + (got[1] + got[2])
            shift += 2
    return value


def conductances(sig_pad):
    full = jnp.pad(sig_pad, ((0, 0), (0, 0), (1, 1)))
    cond_x = 0.5 * (full[1:, 1:-1, 1:-1] + full[:-1, 1:-1, 1:-1])
    cond_y = 0.5 * (full[1:-1, 1:, 1:-1] + full[1:-1, :-1, 1:-1])
    cond_z = 0.5 * (full[1:-1, 1:-1, 1:] + full[1:-1, 1:-1, :-1])
    return (cond_x, cond_y, cond_z)


def operator(padded, conds):
    full = jnp.pad(padded, ((0, 0), (0, 0), (0, 0), (1, 1)))
    flux_x = conds[0] * (full[:, 1:, 1:-1, 1:-1] - full[:, :-1, 1:-1, 1:-1])
    flux_y = conds[1] * (full[:, 1:-1, 1:, 1:-1] - full[:, 1:-1, :-1, 1:-1])
    flux_z = conds[2] * (full[:, 1:-1, 1:-1, 1:] - full[:, 1:-1, 1:-1, :-1])
    return (
        flux_x[:, :-1]
        - flux_x[:, 1:]
        + (flux_y[:, :, :-1] - flux_y[:, :, 1:])
        + (flux_z[..., :-1] - flux_z[..., 1:])
    )


def gram_of(left, right):
    return jnp.einsum("axyz,bxyz->ab", left, right, precision=lax.Precision.HIGHEST)


def combine_cols(field, matrix):
    return jnp.einsum("axyz,ab->bxyz", field, matrix, precision=lax.Precision.HIGHEST)


def posdef_solve(matrix, right):
    lower = jnp.linalg.cholesky(matrix)
    middle = lax.linalg.triangular_solve(lower, right, left_side=True, lower=True)
    return lax.linalg.triangular_solve(lower, middle, left_side=True, lower=True, transpose_a=True)


def one_hot(cells, start, count):
    return (cells[:, None] == start + jnp.arange(count, dtype=jnp.int32)[None, :]).astype(
        jnp.float32
    )


def face_terms(field_pad, adjoint_pad):
    fu = jnp.pad(field_pad, ((0, 0), (0, 0), (0, 0), (1, 1)))
    fl = jnp.pad(adjoint_pad, ((0, 0), (0, 0), (0, 0), (1, 1)))
    term_x = jnp.sum(
        (fu[:, 1:, 1:-1, 1:-1] - fu[:, :-1, 1:-1, 1:-1])
        * (fl[:, 1:, 1:-1, 1:-1] - fl[:, :-1, 1:-1, 1:-1]),
        axis=0,
    )
    term_y = jnp.sum(
        (fu[:, 1:-1, 1:, 1:-1] - fu[:, 1:-1, :-1, 1:-1])
        * (fl[:, 1:-1, 1:, 1:-1] - fl[:, 1:-1, :-1, 1:-1]),
        axis=0,
    )
    term_z = jnp.sum(
        (fu[:, 1:-1, 1:-1, 1:] - fu[:, 1:-1, 1:-1, :-1])
        * (fl[:, 1:-1, 1:-1, 1:] - fl[:, 1:-1, 1:-1, :-1]),
        axis=0,
    )
    return (term_x, term_y, term_z)


HI = lax.Precision.HIGHEST

def _mm(a, b):
    return jnp.dot(a, b, precision=HI, preferred_element_type=jnp.float32)

def _tr(a):
    return jnp.transpose(a)

def _solve(pairs, unroll):
    n = pairs[0][0].shape[0]
    shape = pairs[0][0].shape
    rows = lax.broadcasted_iota(jnp.int32, shape, 0)
    lanes = lax.broadcasted_iota(jnp.int32, shape, 1)
    lane_r = lax.broadcasted_iota(jnp.int32, (1, n), 1)

    def step(j, carry):
        pick = rows == j
        out = []
        for m, r in carry:
            row_m = jnp.sum(jnp.where(pick, m, 0.0), axis=0, keepdims=True)
            row_r = jnp.sum(jnp.where(pick, r, 0.0), axis=0, keepdims=True)
            pivot = jnp.sum(jnp.where(lane_r == j, row_m, 0.0), axis=1, keepdims=True)
            col = jnp.sum(jnp.where(lanes == j, m, 0.0), axis=1, keepdims=True)
            row_m = row_m / pivot
            row_r = row_r / pivot
            m = jnp.where(pick, row_m, m - col * row_m)
            r = jnp.where(pick, row_r, r - col * row_r)
            out.append((m, r))
        return tuple(out)

    done = lax.fori_loop(0, n, step, tuple(pairs), unroll=unroll)
    return [r for _, r in done]


def steps_kernel(grams_ref, out_ref):
    g_rr = grams_ref[0]
    g_rq = grams_ref[1]
    g_qq = grams_ref[2]
    g_qw = grams_ref[3]
    n = g_rr.shape[0]
    eye = (
        lax.broadcasted_iota(jnp.int32, (n, n), 0) == lax.broadcasted_iota(jnp.int32, (n, n), 1)
    ).astype(jnp.float32)
    step0, rr_inv = _solve([(g_rq, g_rr), (g_rr, eye)], 2)
    cross = _mm(g_rq, step0)
    step0_t = _tr(step0)
    new_gram = g_rr - cross - _tr(cross) + _mm(step0_t, _mm(g_qq, step0))
    turn = _mm(rr_inv, new_gram)
    keep = eye + turn
    keep_t = _tr(keep)
    curv = (
        _mm(keep_t, _mm(g_rq, keep))
        - _mm(keep_t, _mm(g_qq, step0))
        - _mm(step0_t, _mm(g_qq, keep))
        + _mm(step0_t, _mm(g_qw, step0))
    )
    (step1,) = _solve([(curv, new_gram)], 4)
    out_ref[0] = step0 + _mm(keep, step1)
    out_ref[1] = -_mm(step0, step1)


def steps(grams):
    n = grams.shape[1]
    return pl.pallas_call(
        steps_kernel,
        out_shape=jax.ShapeDtypeStruct((2, n, n), jnp.float32),
        cost_estimate=pl.CostEstimate(flops=20_000_000_000, transcendentals=0, bytes_accessed=6 * n * n * 4),
    )(grams)


def on_device(conductivity, electrodes, pair_order, initial_fields, adjoint_fields):
    cells_x, cells_y, cells_z = conductivity.shape
    columns = initial_fields.shape[0]
    total_y = lax.axis_size("gy") * cells_y
    start_x = lax.axis_index("gx") * cells_x
    start_y = lax.axis_index("gy") * cells_y
    picked = jnp.take(electrodes, pair_order, axis=0)

    def point_source(flat):
        xs = flat // (total_y * cells_z)
        ys = flat // cells_z % total_y
        zs = flat % cells_z
        return jnp.einsum(
            "cx,cy,cz->cxyz",
            one_hot(xs, start_x, cells_x),
            one_hot(ys, start_y, cells_y),
            one_hot(zs, 0, cells_z),
        )

    right = INJECT * (point_source(picked[:, 0]) - point_source(picked[:, 1]))
    sides = (("gx", 1), ("gy", 2))
    grid_axes = ("gx", "gy")
    stacked = jnp.concatenate([conductivity[None], initial_fields], axis=0)
    padded = padded_2(stacked, sides, 1)
    conds = conductances(padded[0])
    iter_pad = padded[1:]
    residual = right - operator(iter_pad, conds)
    res_pad = padded_2(residual, sides, 1)
    image = operator(res_pad, conds)
    image_pad = padded_2(image, sides, 1)
    image2 = operator(image_pad, conds)
    image2, adjoint_late = lax.optimization_barrier((image2, adjoint_fields))
    adjoint_pad = padded_2(adjoint_late, sides, 1)
    grams = allsum(
        jnp.stack(
            [
                gram_of(residual, residual),
                gram_of(residual, image),
                gram_of(image, image),
                gram_of(image, image2),
            ]
        ),
        grid_axes,
    )

    solved = steps(grams)
    it2_pad = iter_pad + combine_cols(res_pad, solved[0]) + combine_cols(image_pad, solved[1])
    iterate = it2_pad[:, 1:-1, 1:-1]
    term_x, term_y, term_z = face_terms(it2_pad, adjoint_pad)
    local_grad = (
        -0.5
        / columns
        * (
            term_x[:-1]
            + term_x[1:]
            + term_y[:, :-1]
            + term_y[:, 1:]
            + term_z[..., :-1]
            + term_z[..., 1:]
        )
    )
    groups = lax.axis_size("src")
    share = cells_z // groups
    own = lax.axis_index("src")
    if groups == 2:
        other = 1 - own
        sent = lax.dynamic_slice_in_dim(local_grad, other * share, share, 2)
        got = lax.ppermute(sent, "src", [(0, 1), (1, 0)])
        gradient = lax.dynamic_slice_in_dim(local_grad, own * share, share, 2) + got
    else:
        summed = lax.psum(local_grad, "src")
        gradient = lax.dynamic_slice_in_dim(summed, own * share, share, 2)
    return (iterate, gradient)


def solution(mesh):
    placed = (
        P("gx", "gy", None),
        P(),
        P("src"),
        P("src", "gx", "gy", None),
        P("src", "gx", "gy", None),
    )
    return jax.shard_map(
        on_device,
        mesh=mesh,
        in_specs=placed,
        out_specs=(P("src", "gx", "gy", None), P("gx", "gy", "src")),
        check_vma=False,
    )
```

```python
import jax
import jax.numpy as jnp
from jax import lax
from jax.sharding import PartitionSpec as P
from jax.experimental import pallas as pl

ITERS = 2


INJECT = 4.0


def padded_2(block, sides, width):
    (axis_x, dim_x), (axis_y, dim_y) = sides
    pieces = {}
    for axis, dim in sides:
        count = lax.axis_size(axis)
        place = lax.axis_index(axis)
        forward = [(i, (i + 1) % count) for i in range(count)]
        backward = [(target, source) for source, target in forward]
        top = lax.slice_in_dim(block, block.shape[dim] - width, None, axis=dim)
        bottom = lax.slice_in_dim(block, 0, width, axis=dim)
        top = jnp.where(place == count - 1, jnp.zeros_like(top), top)
        bottom = jnp.where(place == 0, jnp.zeros_like(bottom), bottom)
        low = lax.ppermute(top, axis, forward)
        high = lax.ppermute(bottom, axis, backward)
        pieces[axis] = (low, high)
    low_x, high_x = pieces[axis_x]
    low_y, high_y = pieces[axis_y]
    middle = jnp.concatenate([low_x, block, high_x], axis=dim_x)
    rim = [(0, 0)] * block.ndim
    rim[dim_x] = (width, width)
    low_y = jnp.pad(low_y, rim)
    high_y = jnp.pad(high_y, rim)
    return jnp.concatenate([low_y, middle, high_y], axis=dim_y)


def allsum(value, axes):
    for axis in axes:
        count = lax.axis_size(axis)
        if count & (count - 1):
            value = lax.psum(value, axis)
            continue
        shift = 0
        if (count.bit_length() - 1) % 2:
            value = value + lax.ppermute(value, axis, [(i, i ^ 1) for i in range(count)])
            shift = 1
        while (1 << shift) < count:
            got = [
                lax.ppermute(value, axis, [(i, i ^ (d << shift)) for i in range(count)])
                for d in (1, 2, 3)
            ]
            value = (value + got[0]) + (got[1] + got[2])
            shift += 2
    return value


def conductances(sig_pad):
    full = jnp.pad(sig_pad, ((0, 0), (0, 0), (1, 1)))
    cond_x = 0.5 * (full[1:, 1:-1, 1:-1] + full[:-1, 1:-1, 1:-1])
    cond_y = 0.5 * (full[1:-1, 1:, 1:-1] + full[1:-1, :-1, 1:-1])
    cond_z = 0.5 * (full[1:-1, 1:-1, 1:] + full[1:-1, 1:-1, :-1])
    return (cond_x, cond_y, cond_z)


def operator(padded, conds):
    full = jnp.pad(padded, ((0, 0), (0, 0), (0, 0), (1, 1)))
    flux_x = conds[0] * (full[:, 1:, 1:-1, 1:-1] - full[:, :-1, 1:-1, 1:-1])
    flux_y = conds[1] * (full[:, 1:-1, 1:, 1:-1] - full[:, 1:-1, :-1, 1:-1])
    flux_z = conds[2] * (full[:, 1:-1, 1:-1, 1:] - full[:, 1:-1, 1:-1, :-1])
    return (
        flux_x[:, :-1]
        - flux_x[:, 1:]
        + (flux_y[:, :, :-1] - flux_y[:, :, 1:])
        + (flux_z[..., :-1] - flux_z[..., 1:])
    )


def gram_of(left, right):
    return jnp.einsum("axyz,bxyz->ab", left, right, precision=lax.Precision.HIGHEST)


def combine_cols(field, matrix):
    return jnp.einsum("axyz,ab->bxyz", field, matrix, precision=lax.Precision.HIGHEST)


def posdef_solve(matrix, right):
    lower = jnp.linalg.cholesky(matrix)
    middle = lax.linalg.triangular_solve(lower, right, left_side=True, lower=True)
    return lax.linalg.triangular_solve(lower, middle, left_side=True, lower=True, transpose_a=True)


def one_hot(cells, start, count):
    return (cells[:, None] == start + jnp.arange(count, dtype=jnp.int32)[None, :]).astype(
        jnp.float32
    )


def face_terms(field_pad, adjoint_pad):
    fu = jnp.pad(field_pad, ((0, 0), (0, 0), (0, 0), (1, 1)))
    fl = jnp.pad(adjoint_pad, ((0, 0), (0, 0), (0, 0), (1, 1)))
    term_x = jnp.sum(
        (fu[:, 1:, 1:-1, 1:-1] - fu[:, :-1, 1:-1, 1:-1])
        * (fl[:, 1:, 1:-1, 1:-1] - fl[:, :-1, 1:-1, 1:-1]),
        axis=0,
    )
    term_y = jnp.sum(
        (fu[:, 1:-1, 1:, 1:-1] - fu[:, 1:-1, :-1, 1:-1])
        * (fl[:, 1:-1, 1:, 1:-1] - fl[:, 1:-1, :-1, 1:-1]),
        axis=0,
    )
    term_z = jnp.sum(
        (fu[:, 1:-1, 1:-1, 1:] - fu[:, 1:-1, 1:-1, :-1])
        * (fl[:, 1:-1, 1:-1, 1:] - fl[:, 1:-1, 1:-1, :-1]),
        axis=0,
    )
    return (term_x, term_y, term_z)


HI = lax.Precision.HIGHEST

def _mm(a, b):
    return jnp.dot(a, b, precision=HI, preferred_element_type=jnp.float32)

def _tr(a):
    return jnp.transpose(a)

def _solve(pairs, unroll):
    n = pairs[0][0].shape[0]
    shape = pairs[0][0].shape
    rows = lax.broadcasted_iota(jnp.int32, shape, 0)
    lanes = lax.broadcasted_iota(jnp.int32, shape, 1)
    lane_r = lax.broadcasted_iota(jnp.int32, (1, n), 1)

    def step(j, carry):
        pick = rows == j
        out = []
        for m, r in carry:
            row_m = jnp.sum(jnp.where(pick, m, 0.0), axis=0, keepdims=True)
            row_r = jnp.sum(jnp.where(pick, r, 0.0), axis=0, keepdims=True)
            pivot = jnp.sum(jnp.where(lane_r == j, row_m, 0.0), axis=1, keepdims=True)
            col = jnp.sum(jnp.where(lanes == j, m, 0.0), axis=1, keepdims=True)
            scale = 1.0 / pivot
            row_m = row_m * scale
            row_r = row_r * scale
            m = jnp.where(pick, row_m, m - col * row_m)
            r = jnp.where(pick, row_r, r - col * row_r)
            out.append((m, r))
        return tuple(out)

    done = lax.fori_loop(0, n, step, tuple(pairs), unroll=unroll)
    return [r for _, r in done]


def steps_kernel(grams_ref, out_ref):
    g_rr = grams_ref[0]
    g_rq = grams_ref[1]
    g_qq = grams_ref[2]
    g_qw = grams_ref[3]
    n = g_rr.shape[0]
    eye = (
        lax.broadcasted_iota(jnp.int32, (n, n), 0) == lax.broadcasted_iota(jnp.int32, (n, n), 1)
    ).astype(jnp.float32)
    step0, rr_inv = _solve([(g_rq, g_rr), (g_rr, eye)], True)
    cross = _mm(g_rq, step0)
    step0_t = _tr(step0)
    new_gram = g_rr - cross - _tr(cross) + _mm(step0_t, _mm(g_qq, step0))
    turn = _mm(rr_inv, new_gram)
    keep = eye + turn
    keep_t = _tr(keep)
    curv = (
        _mm(keep_t, _mm(g_rq, keep))
        - _mm(keep_t, _mm(g_qq, step0))
        - _mm(step0_t, _mm(g_qq, keep))
        + _mm(step0_t, _mm(g_qw, step0))
    )
    (step1,) = _solve([(curv, new_gram)], True)
    out_ref[0] = step0 + _mm(keep, step1)
    out_ref[1] = -_mm(step0, step1)


def steps(grams):
    n = grams.shape[1]
    return pl.pallas_call(
        steps_kernel,
        out_shape=jax.ShapeDtypeStruct((2, n, n), jnp.float32),
        cost_estimate=pl.CostEstimate(flops=20_000_000_000, transcendentals=0, bytes_accessed=6 * n * n * 4),
    )(grams)


def on_device(conductivity, electrodes, pair_order, initial_fields, adjoint_fields):
    cells_x, cells_y, cells_z = conductivity.shape
    columns = initial_fields.shape[0]
    total_y = lax.axis_size("gy") * cells_y
    start_x = lax.axis_index("gx") * cells_x
    start_y = lax.axis_index("gy") * cells_y
    picked = jnp.take(electrodes, pair_order, axis=0)

    def point_source(flat):
        xs = flat // (total_y * cells_z)
        ys = flat // cells_z % total_y
        zs = flat % cells_z
        return jnp.einsum(
            "cx,cy,cz->cxyz",
            one_hot(xs, start_x, cells_x),
            one_hot(ys, start_y, cells_y),
            one_hot(zs, 0, cells_z),
        )

    right = INJECT * (point_source(picked[:, 0]) - point_source(picked[:, 1]))
    sides = (("gx", 1), ("gy", 2))
    grid_axes = ("gx", "gy")
    stacked = jnp.concatenate([conductivity[None], initial_fields], axis=0)
    padded = padded_2(stacked, sides, 1)
    conds = conductances(padded[0])
    iter_pad = padded[1:]
    residual = right - operator(iter_pad, conds)
    res_pad = padded_2(residual, sides, 1)
    image = operator(res_pad, conds)
    image_pad = padded_2(image, sides, 1)
    image2 = operator(image_pad, conds)
    image2, adjoint_late = lax.optimization_barrier((image2, adjoint_fields))
    adjoint_pad = padded_2(adjoint_late, sides, 1)
    grams = allsum(
        jnp.stack(
            [
                gram_of(residual, residual),
                gram_of(residual, image),
                gram_of(image, image),
                gram_of(image, image2),
            ]
        ),
        grid_axes,
    )

    solved = steps(grams)
    it2_pad = iter_pad + combine_cols(res_pad, solved[0]) + combine_cols(image_pad, solved[1])
    iterate = it2_pad[:, 1:-1, 1:-1]
    term_x, term_y, term_z = face_terms(it2_pad, adjoint_pad)
    local_grad = (
        -0.5
        / columns
        * (
            term_x[:-1]
            + term_x[1:]
            + term_y[:, :-1]
            + term_y[:, 1:]
            + term_z[..., :-1]
            + term_z[..., 1:]
        )
    )
    groups = lax.axis_size("src")
    share = cells_z // groups
    own = lax.axis_index("src")
    if groups == 2:
        other = 1 - own
        sent = lax.dynamic_slice_in_dim(local_grad, other * share, share, 2)
        got = lax.ppermute(sent, "src", [(0, 1), (1, 0)])
        gradient = lax.dynamic_slice_in_dim(local_grad, own * share, share, 2) + got
    else:
        summed = lax.psum(local_grad, "src")
        gradient = lax.dynamic_slice_in_dim(summed, own * share, share, 2)
    return (iterate, gradient)


def solution(mesh):
    placed = (
        P("gx", "gy", None),
        P(),
        P("src"),
        P("src", "gx", "gy", None),
        P("src", "gx", "gy", None),
    )
    return jax.shard_map(
        on_device,
        mesh=mesh,
        in_specs=placed,
        out_specs=(P("src", "gx", "gy", None), P("gx", "gy", "src")),
        check_vma=False,
    )
```

```python
import jax
import jax.numpy as jnp
from jax import lax
from jax.sharding import PartitionSpec as P
from jax.experimental import pallas as pl

ITERS = 2


INJECT = 4.0


def padded_2(block, sides, width):
    (axis_x, dim_x), (axis_y, dim_y) = sides
    pieces = {}
    for axis, dim in sides:
        count = lax.axis_size(axis)
        place = lax.axis_index(axis)
        forward = [(i, (i + 1) % count) for i in range(count)]
        backward = [(target, source) for source, target in forward]
        top = lax.slice_in_dim(block, block.shape[dim] - width, None, axis=dim)
        bottom = lax.slice_in_dim(block, 0, width, axis=dim)
        top = jnp.where(place == count - 1, jnp.zeros_like(top), top)
        bottom = jnp.where(place == 0, jnp.zeros_like(bottom), bottom)
        low = lax.ppermute(top, axis, forward)
        high = lax.ppermute(bottom, axis, backward)
        pieces[axis] = (low, high)
    low_x, high_x = pieces[axis_x]
    low_y, high_y = pieces[axis_y]
    middle = jnp.concatenate([low_x, block, high_x], axis=dim_x)
    rim = [(0, 0)] * block.ndim
    rim[dim_x] = (width, width)
    low_y = jnp.pad(low_y, rim)
    high_y = jnp.pad(high_y, rim)
    return jnp.concatenate([low_y, middle, high_y], axis=dim_y)


def allsum(value, axes):
    for axis in axes:
        count = lax.axis_size(axis)
        if count & (count - 1):
            value = lax.psum(value, axis)
            continue
        shift = 0
        if (count.bit_length() - 1) % 2:
            value = value + lax.ppermute(value, axis, [(i, i ^ 1) for i in range(count)])
            shift = 1
        while (1 << shift) < count:
            got = [
                lax.ppermute(value, axis, [(i, i ^ (d << shift)) for i in range(count)])
                for d in (1, 2, 3)
            ]
            value = (value + got[0]) + (got[1] + got[2])
            shift += 2
    return value


def conductances(sig_pad):
    full = jnp.pad(sig_pad, ((0, 0), (0, 0), (1, 1)))
    cond_x = 0.5 * (full[1:, 1:-1, 1:-1] + full[:-1, 1:-1, 1:-1])
    cond_y = 0.5 * (full[1:-1, 1:, 1:-1] + full[1:-1, :-1, 1:-1])
    cond_z = 0.5 * (full[1:-1, 1:-1, 1:] + full[1:-1, 1:-1, :-1])
    return (cond_x, cond_y, cond_z)


def operator(padded, conds):
    full = jnp.pad(padded, ((0, 0), (0, 0), (0, 0), (1, 1)))
    flux_x = conds[0] * (full[:, 1:, 1:-1, 1:-1] - full[:, :-1, 1:-1, 1:-1])
    flux_y = conds[1] * (full[:, 1:-1, 1:, 1:-1] - full[:, 1:-1, :-1, 1:-1])
    flux_z = conds[2] * (full[:, 1:-1, 1:-1, 1:] - full[:, 1:-1, 1:-1, :-1])
    return (
        flux_x[:, :-1]
        - flux_x[:, 1:]
        + (flux_y[:, :, :-1] - flux_y[:, :, 1:])
        + (flux_z[..., :-1] - flux_z[..., 1:])
    )


def gram_of(left, right):
    return jnp.einsum("axyz,bxyz->ab", left, right, precision=lax.Precision.HIGHEST)


def combine_cols(field, matrix):
    return jnp.einsum("axyz,ab->bxyz", field, matrix, precision=lax.Precision.HIGHEST)


def posdef_solve(matrix, right):
    lower = jnp.linalg.cholesky(matrix)
    middle = lax.linalg.triangular_solve(lower, right, left_side=True, lower=True)
    return lax.linalg.triangular_solve(lower, middle, left_side=True, lower=True, transpose_a=True)


def one_hot(cells, start, count):
    return (cells[:, None] == start + jnp.arange(count, dtype=jnp.int32)[None, :]).astype(
        jnp.float32
    )


def face_terms(field_pad, adjoint_pad):
    fu = jnp.pad(field_pad, ((0, 0), (0, 0), (0, 0), (1, 1)))
    fl = jnp.pad(adjoint_pad, ((0, 0), (0, 0), (0, 0), (1, 1)))
    term_x = jnp.sum(
        (fu[:, 1:, 1:-1, 1:-1] - fu[:, :-1, 1:-1, 1:-1])
        * (fl[:, 1:, 1:-1, 1:-1] - fl[:, :-1, 1:-1, 1:-1]),
        axis=0,
    )
    term_y = jnp.sum(
        (fu[:, 1:-1, 1:, 1:-1] - fu[:, 1:-1, :-1, 1:-1])
        * (fl[:, 1:-1, 1:, 1:-1] - fl[:, 1:-1, :-1, 1:-1]),
        axis=0,
    )
    term_z = jnp.sum(
        (fu[:, 1:-1, 1:-1, 1:] - fu[:, 1:-1, 1:-1, :-1])
        * (fl[:, 1:-1, 1:-1, 1:] - fl[:, 1:-1, 1:-1, :-1]),
        axis=0,
    )
    return (term_x, term_y, term_z)


HI = lax.Precision.HIGHEST

def _mm(a, b):
    return jnp.dot(a, b, precision=HI, preferred_element_type=jnp.float32)

def _tr(a):
    return jnp.transpose(a)

def _solve(pairs, unroll):
    n = pairs[0][0].shape[0]
    shape = pairs[0][0].shape
    rows = lax.broadcasted_iota(jnp.int32, shape, 0)
    lanes = lax.broadcasted_iota(jnp.int32, shape, 1)
    lane_r = lax.broadcasted_iota(jnp.int32, (1, n), 1)

    def step(j, carry):
        pick = rows == j
        out = []
        for m, r in carry:
            row_m = jnp.sum(jnp.where(pick, m, 0.0), axis=0, keepdims=True)
            row_r = jnp.sum(jnp.where(pick, r, 0.0), axis=0, keepdims=True)
            pivot = jnp.sum(jnp.where(lane_r == j, row_m, 0.0), axis=1, keepdims=True)
            col = jnp.sum(jnp.where(lanes == j, m, 0.0), axis=1, keepdims=True)
            scale = 1.0 / pivot
            row_m = row_m * scale
            row_r = row_r * scale
            m = jnp.where(pick, row_m, m - col * row_m)
            r = jnp.where(pick, row_r, r - col * row_r)
            out.append((m, r))
        return tuple(out)

    done = lax.fori_loop(0, n, step, tuple(pairs), unroll=unroll)
    return [r for _, r in done]


def first_kernel(grams_ref, out_ref):
    g_rr = grams_ref[0]
    g_rq = grams_ref[1]
    g_qq = grams_ref[2]
    n = g_rr.shape[0]
    eye = (
        lax.broadcasted_iota(jnp.int32, (n, n), 0) == lax.broadcasted_iota(jnp.int32, (n, n), 1)
    ).astype(jnp.float32)
    step0, rr_inv = _solve([(g_rq, g_rr), (g_rr, eye)], True)
    cross = _mm(g_rq, step0)
    new_gram = g_rr - cross - _tr(cross) + _mm(_tr(step0), _mm(g_qq, step0))
    out_ref[0] = step0
    out_ref[1] = _mm(rr_inv, new_gram)
    out_ref[2] = new_gram


def second_kernel(grams_ref, first_ref, last_ref, out_ref):
    g_rq = grams_ref[1]
    g_qq = grams_ref[2]
    g_qw = last_ref[0]
    step0 = first_ref[0]
    turn = first_ref[1]
    new_gram = first_ref[2]
    n = g_rq.shape[0]
    eye = (
        lax.broadcasted_iota(jnp.int32, (n, n), 0) == lax.broadcasted_iota(jnp.int32, (n, n), 1)
    ).astype(jnp.float32)
    step0_t = _tr(step0)
    keep = eye + turn
    keep_t = _tr(keep)
    curv = (
        _mm(keep_t, _mm(g_rq, keep))
        - _mm(keep_t, _mm(g_qq, step0))
        - _mm(step0_t, _mm(g_qq, keep))
        + _mm(step0_t, _mm(g_qw, step0))
    )
    (step1,) = _solve([(curv, new_gram)], True)
    out_ref[0] = step0 + _mm(keep, step1)
    out_ref[1] = -_mm(step0, step1)


def steps(grams, last):
    n = grams.shape[1]
    first = pl.pallas_call(
        first_kernel,
        out_shape=jax.ShapeDtypeStruct((3, n, n), jnp.float32),
        cost_estimate=pl.CostEstimate(flops=10_000_000_000, transcendentals=0, bytes_accessed=6 * n * n * 4),
    )(grams)
    return pl.pallas_call(
        second_kernel,
        out_shape=jax.ShapeDtypeStruct((2, n, n), jnp.float32),
        cost_estimate=pl.CostEstimate(flops=10_000_000_000, transcendentals=0, bytes_accessed=9 * n * n * 4),
    )(grams, first, last)


def on_device(conductivity, electrodes, pair_order, initial_fields, adjoint_fields):
    cells_x, cells_y, cells_z = conductivity.shape
    columns = initial_fields.shape[0]
    total_y = lax.axis_size("gy") * cells_y
    start_x = lax.axis_index("gx") * cells_x
    start_y = lax.axis_index("gy") * cells_y
    picked = jnp.take(electrodes, pair_order, axis=0)

    def point_source(flat):
        xs = flat // (total_y * cells_z)
        ys = flat // cells_z % total_y
        zs = flat % cells_z
        return jnp.einsum(
            "cx,cy,cz->cxyz",
            one_hot(xs, start_x, cells_x),
            one_hot(ys, start_y, cells_y),
            one_hot(zs, 0, cells_z),
        )

    right = INJECT * (point_source(picked[:, 0]) - point_source(picked[:, 1]))
    sides = (("gx", 1), ("gy", 2))
    grid_axes = ("gx", "gy")
    stacked = jnp.concatenate([conductivity[None], initial_fields], axis=0)
    padded = padded_2(stacked, sides, 1)
    conds = conductances(padded[0])
    iter_pad = padded[1:]
    residual = right - operator(iter_pad, conds)
    res_pad = padded_2(residual, sides, 1)
    image = operator(res_pad, conds)
    grams = allsum(
        jnp.stack(
            [
                gram_of(residual, residual),
                gram_of(residual, image),
                gram_of(image, image),
            ]
        ),
        grid_axes,
    )
    image_pad = padded_2(image, sides, 1)
    image2 = operator(image_pad, conds)
    image2, adjoint_late = lax.optimization_barrier((image2, adjoint_fields))
    adjoint_pad = padded_2(adjoint_late, sides, 1)
    last = allsum(gram_of(image, image2)[None], grid_axes)
    solved = steps(grams, last)
    it2_pad = iter_pad + combine_cols(res_pad, solved[0]) + combine_cols(image_pad, solved[1])
    iterate = it2_pad[:, 1:-1, 1:-1]
    term_x, term_y, term_z = face_terms(it2_pad, adjoint_pad)
    local_grad = (
        -0.5
        / columns
        * (
            term_x[:-1]
            + term_x[1:]
            + term_y[:, :-1]
            + term_y[:, 1:]
            + term_z[..., :-1]
            + term_z[..., 1:]
        )
    )
    groups = lax.axis_size("src")
    share = cells_z // groups
    own = lax.axis_index("src")
    if groups == 2:
        other = 1 - own
        sent = lax.dynamic_slice_in_dim(local_grad, other * share, share, 2)
        got = lax.ppermute(sent, "src", [(0, 1), (1, 0)])
        gradient = lax.dynamic_slice_in_dim(local_grad, own * share, share, 2) + got
    else:
        summed = lax.psum(local_grad, "src")
        gradient = lax.dynamic_slice_in_dim(summed, own * share, share, 2)
    return (iterate, gradient)


def solution(mesh):
    placed = (
        P("gx", "gy", None),
        P(),
        P("src"),
        P("src", "gx", "gy", None),
        P("src", "gx", "gy", None),
    )
    return jax.shard_map(
        on_device,
        mesh=mesh,
        in_specs=placed,
        out_specs=(P("src", "gx", "gy", None), P("gx", "gy", "src")),
        check_vma=False,
    )
```

```python
import jax
import jax.numpy as jnp
from jax import lax
from jax.sharding import PartitionSpec as P
from jax.experimental import pallas as pl

ITERS = 2


INJECT = 4.0


def padded_2(block, sides, width):
    (axis_x, dim_x), (axis_y, dim_y) = sides
    pieces = {}
    for axis, dim in sides:
        count = lax.axis_size(axis)
        place = lax.axis_index(axis)
        forward = [(i, (i + 1) % count) for i in range(count)]
        backward = [(target, source) for source, target in forward]
        top = lax.slice_in_dim(block, block.shape[dim] - width, None, axis=dim)
        bottom = lax.slice_in_dim(block, 0, width, axis=dim)
        top = jnp.where(place == count - 1, jnp.zeros_like(top), top)
        bottom = jnp.where(place == 0, jnp.zeros_like(bottom), bottom)
        low = lax.ppermute(top, axis, forward)
        high = lax.ppermute(bottom, axis, backward)
        pieces[axis] = (low, high)
    low_x, high_x = pieces[axis_x]
    low_y, high_y = pieces[axis_y]
    middle = jnp.concatenate([low_x, block, high_x], axis=dim_x)
    rim = [(0, 0)] * block.ndim
    rim[dim_x] = (width, width)
    low_y = jnp.pad(low_y, rim)
    high_y = jnp.pad(high_y, rim)
    return jnp.concatenate([low_y, middle, high_y], axis=dim_y)


def allsum(value, axes):
    for axis in axes:
        count = lax.axis_size(axis)
        if count & (count - 1):
            value = lax.psum(value, axis)
            continue
        shift = 0
        if (count.bit_length() - 1) % 2:
            value = value + lax.ppermute(value, axis, [(i, i ^ 1) for i in range(count)])
            shift = 1
        while (1 << shift) < count:
            got = [
                lax.ppermute(value, axis, [(i, i ^ (d << shift)) for i in range(count)])
                for d in (1, 2, 3)
            ]
            value = (value + got[0]) + (got[1] + got[2])
            shift += 2
    return value


def conductances(sig_pad):
    full = jnp.pad(sig_pad, ((0, 0), (0, 0), (1, 1)))
    cond_x = 0.5 * (full[1:, 1:-1, 1:-1] + full[:-1, 1:-1, 1:-1])
    cond_y = 0.5 * (full[1:-1, 1:, 1:-1] + full[1:-1, :-1, 1:-1])
    cond_z = 0.5 * (full[1:-1, 1:-1, 1:] + full[1:-1, 1:-1, :-1])
    return (cond_x, cond_y, cond_z)


def operator(padded, conds):
    full = jnp.pad(padded, ((0, 0), (0, 0), (0, 0), (1, 1)))
    flux_x = conds[0] * (full[:, 1:, 1:-1, 1:-1] - full[:, :-1, 1:-1, 1:-1])
    flux_y = conds[1] * (full[:, 1:-1, 1:, 1:-1] - full[:, 1:-1, :-1, 1:-1])
    flux_z = conds[2] * (full[:, 1:-1, 1:-1, 1:] - full[:, 1:-1, 1:-1, :-1])
    return (
        flux_x[:, :-1]
        - flux_x[:, 1:]
        + (flux_y[:, :, :-1] - flux_y[:, :, 1:])
        + (flux_z[..., :-1] - flux_z[..., 1:])
    )


def gram_of(left, right):
    return jnp.einsum("axyz,bxyz->ab", left, right, precision=lax.Precision.HIGHEST)


def combine_cols(field, matrix):
    return jnp.einsum("axyz,ab->bxyz", field, matrix, precision=lax.Precision.HIGHEST)


def posdef_solve(matrix, right):
    lower = jnp.linalg.cholesky(matrix)
    middle = lax.linalg.triangular_solve(lower, right, left_side=True, lower=True)
    return lax.linalg.triangular_solve(lower, middle, left_side=True, lower=True, transpose_a=True)


def one_hot(cells, start, count):
    return (cells[:, None] == start + jnp.arange(count, dtype=jnp.int32)[None, :]).astype(
        jnp.float32
    )


def face_terms(field_pad, adjoint_pad):
    fu = jnp.pad(field_pad, ((0, 0), (0, 0), (0, 0), (1, 1)))
    fl = jnp.pad(adjoint_pad, ((0, 0), (0, 0), (0, 0), (1, 1)))
    term_x = jnp.sum(
        (fu[:, 1:, 1:-1, 1:-1] - fu[:, :-1, 1:-1, 1:-1])
        * (fl[:, 1:, 1:-1, 1:-1] - fl[:, :-1, 1:-1, 1:-1]),
        axis=0,
    )
    term_y = jnp.sum(
        (fu[:, 1:-1, 1:, 1:-1] - fu[:, 1:-1, :-1, 1:-1])
        * (fl[:, 1:-1, 1:, 1:-1] - fl[:, 1:-1, :-1, 1:-1]),
        axis=0,
    )
    term_z = jnp.sum(
        (fu[:, 1:-1, 1:-1, 1:] - fu[:, 1:-1, 1:-1, :-1])
        * (fl[:, 1:-1, 1:-1, 1:] - fl[:, 1:-1, 1:-1, :-1]),
        axis=0,
    )
    return (term_x, term_y, term_z)


HI = lax.Precision.HIGHEST

def _mm(a, b):
    return jnp.dot(a, b, precision=HI, preferred_element_type=jnp.float32)

def _tr(a):
    return jnp.transpose(a)

def _solve(pairs, unroll):
    n = pairs[0][0].shape[0]
    shape = pairs[0][0].shape
    rows = lax.broadcasted_iota(jnp.int32, shape, 0)
    lanes = lax.broadcasted_iota(jnp.int32, shape, 1)
    lane_r = lax.broadcasted_iota(jnp.int32, (1, n), 1)

    def pick_row(x, i):
        return jnp.sum(jnp.where(rows == i, x, 0.0), axis=0, keepdims=True)

    def pick_col(x, i):
        return jnp.sum(jnp.where(lanes == i, x, 0.0), axis=1, keepdims=True)

    def entry(row, i):
        return jnp.sum(jnp.where(lane_r == i, row, 0.0), axis=1, keepdims=True)

    def step(k, carry):
        p = 2 * k
        q = p + 1
        out = []
        for m, r in carry:
            row_p = pick_row(m, p)
            row_q = pick_row(m, q)
            res_p = pick_row(r, p)
            res_q = pick_row(r, q)
            col_p = pick_col(m, p)
            col_q = pick_col(m, q)
            a, b = entry(row_p, p), entry(row_p, q)
            c, d = entry(row_q, p), entry(row_q, q)
            scale = 1.0 / (a * d - b * c)
            new_p = (d * row_p - b * row_q) * scale
            new_q = (a * row_q - c * row_p) * scale
            got_p = (d * res_p - b * res_q) * scale
            got_q = (a * res_q - c * res_p) * scale
            m = jnp.where(rows == p, new_p, jnp.where(rows == q, new_q, m - col_p * new_p - col_q * new_q))
            r = jnp.where(rows == p, got_p, jnp.where(rows == q, got_q, r - col_p * got_p - col_q * got_q))
            out.append((m, r))
        return tuple(out)

    done = lax.fori_loop(0, n // 2, step, tuple(pairs), unroll=unroll)
    return [r for _, r in done]


def steps_kernel(grams_ref, out_ref):
    g_rr = grams_ref[0]
    g_rq = grams_ref[1]
    g_qq = grams_ref[2]
    g_qw = grams_ref[3]
    n = g_rr.shape[0]
    eye = (
        lax.broadcasted_iota(jnp.int32, (n, n), 0) == lax.broadcasted_iota(jnp.int32, (n, n), 1)
    ).astype(jnp.float32)
    step0, rr_inv = _solve([(g_rq, g_rr), (g_rr, eye)], True)
    cross = _mm(g_rq, step0)
    step0_t = _tr(step0)
    new_gram = g_rr - cross - _tr(cross) + _mm(step0_t, _mm(g_qq, step0))
    turn = _mm(rr_inv, new_gram)
    keep = eye + turn
    keep_t = _tr(keep)
    curv = (
        _mm(keep_t, _mm(g_rq, keep))
        - _mm(keep_t, _mm(g_qq, step0))
        - _mm(step0_t, _mm(g_qq, keep))
        + _mm(step0_t, _mm(g_qw, step0))
    )
    (step1,) = _solve([(curv, new_gram)], True)
    out_ref[0] = step0 + _mm(keep, step1)
    out_ref[1] = -_mm(step0, step1)


def steps(grams):
    n = grams.shape[1]
    return pl.pallas_call(
        steps_kernel,
        out_shape=jax.ShapeDtypeStruct((2, n, n), jnp.float32),
        cost_estimate=pl.CostEstimate(flops=20_000_000_000, transcendentals=0, bytes_accessed=6 * n * n * 4),
    )(grams)


def on_device(conductivity, electrodes, pair_order, initial_fields, adjoint_fields):
    cells_x, cells_y, cells_z = conductivity.shape
    columns = initial_fields.shape[0]
    total_y = lax.axis_size("gy") * cells_y
    start_x = lax.axis_index("gx") * cells_x
    start_y = lax.axis_index("gy") * cells_y
    picked = jnp.take(electrodes, pair_order, axis=0)

    def point_source(flat):
        xs = flat // (total_y * cells_z)
        ys = flat // cells_z % total_y
        zs = flat % cells_z
        return jnp.einsum(
            "cx,cy,cz->cxyz",
            one_hot(xs, start_x, cells_x),
            one_hot(ys, start_y, cells_y),
            one_hot(zs, 0, cells_z),
        )

    right = INJECT * (point_source(picked[:, 0]) - point_source(picked[:, 1]))
    sides = (("gx", 1), ("gy", 2))
    grid_axes = ("gx", "gy")
    stacked = jnp.concatenate([conductivity[None], initial_fields], axis=0)
    padded = padded_2(stacked, sides, 1)
    conds = conductances(padded[0])
    iter_pad = padded[1:]
    residual = right - operator(iter_pad, conds)
    res_pad = padded_2(residual, sides, 1)
    image = operator(res_pad, conds)
    image_pad = padded_2(image, sides, 1)
    image2 = operator(image_pad, conds)
    image2, adjoint_late = lax.optimization_barrier((image2, adjoint_fields))
    adjoint_pad = padded_2(adjoint_late, sides, 1)
    grams = allsum(
        jnp.stack(
            [
                gram_of(residual, residual),
                gram_of(residual, image),
                gram_of(image, image),
                gram_of(image, image2),
            ]
        ),
        grid_axes,
    )

    solved = steps(grams)
    it2_pad = iter_pad + combine_cols(res_pad, solved[0]) + combine_cols(image_pad, solved[1])
    iterate = it2_pad[:, 1:-1, 1:-1]
    term_x, term_y, term_z = face_terms(it2_pad, adjoint_pad)
    local_grad = (
        -0.5
        / columns
        * (
            term_x[:-1]
            + term_x[1:]
            + term_y[:, :-1]
            + term_y[:, 1:]
            + term_z[..., :-1]
            + term_z[..., 1:]
        )
    )
    groups = lax.axis_size("src")
    share = cells_z // groups
    own = lax.axis_index("src")
    if groups == 2:
        other = 1 - own
        sent = lax.dynamic_slice_in_dim(local_grad, other * share, share, 2)
        got = lax.ppermute(sent, "src", [(0, 1), (1, 0)])
        gradient = lax.dynamic_slice_in_dim(local_grad, own * share, share, 2) + got
    else:
        summed = lax.psum(local_grad, "src")
        gradient = lax.dynamic_slice_in_dim(summed, own * share, share, 2)
    return (iterate, gradient)


def solution(mesh):
    placed = (
        P("gx", "gy", None),
        P(),
        P("src"),
        P("src", "gx", "gy", None),
        P("src", "gx", "gy", None),
    )
    return jax.shard_map(
        on_device,
        mesh=mesh,
        in_specs=placed,
        out_specs=(P("src", "gx", "gy", None), P("gx", "gy", "src")),
        check_vma=False,
    )
```

```python
import jax
import jax.numpy as jnp
from jax import lax
from jax.sharding import PartitionSpec as P
from jax.experimental import pallas as pl

ITERS = 2


INJECT = 4.0


def padded_2(block, sides, width):
    (axis_x, dim_x), (axis_y, dim_y) = sides
    pieces = {}
    for axis, dim in sides:
        count = lax.axis_size(axis)
        place = lax.axis_index(axis)
        forward = [(i, (i + 1) % count) for i in range(count)]
        backward = [(target, source) for source, target in forward]
        top = lax.slice_in_dim(block, block.shape[dim] - width, None, axis=dim)
        bottom = lax.slice_in_dim(block, 0, width, axis=dim)
        top = jnp.where(place == count - 1, jnp.zeros_like(top), top)
        bottom = jnp.where(place == 0, jnp.zeros_like(bottom), bottom)
        low = lax.ppermute(top, axis, forward)
        high = lax.ppermute(bottom, axis, backward)
        pieces[axis] = (low, high)
    low_x, high_x = pieces[axis_x]
    low_y, high_y = pieces[axis_y]
    middle = jnp.concatenate([low_x, block, high_x], axis=dim_x)
    rim = [(0, 0)] * block.ndim
    rim[dim_x] = (width, width)
    low_y = jnp.pad(low_y, rim)
    high_y = jnp.pad(high_y, rim)
    return jnp.concatenate([low_y, middle, high_y], axis=dim_y)


def allsum(value, axes):
    for axis in axes:
        count = lax.axis_size(axis)
        if count & (count - 1):
            value = lax.psum(value, axis)
            continue
        shift = 0
        if (count.bit_length() - 1) % 2:
            value = value + lax.ppermute(value, axis, [(i, i ^ 1) for i in range(count)])
            shift = 1
        while (1 << shift) < count:
            got = [
                lax.ppermute(value, axis, [(i, i ^ (d << shift)) for i in range(count)])
                for d in (1, 2, 3)
            ]
            value = (value + got[0]) + (got[1] + got[2])
            shift += 2
    return value


def conductances(sig_pad):
    full = jnp.pad(sig_pad, ((0, 0), (0, 0), (1, 1)))
    cond_x = 0.5 * (full[1:, 1:-1, 1:-1] + full[:-1, 1:-1, 1:-1])
    cond_y = 0.5 * (full[1:-1, 1:, 1:-1] + full[1:-1, :-1, 1:-1])
    cond_z = 0.5 * (full[1:-1, 1:-1, 1:] + full[1:-1, 1:-1, :-1])
    return (cond_x, cond_y, cond_z)


def operator(padded, conds):
    full = jnp.pad(padded, ((0, 0), (0, 0), (0, 0), (1, 1)))
    flux_x = conds[0] * (full[:, 1:, 1:-1, 1:-1] - full[:, :-1, 1:-1, 1:-1])
    flux_y = conds[1] * (full[:, 1:-1, 1:, 1:-1] - full[:, 1:-1, :-1, 1:-1])
    flux_z = conds[2] * (full[:, 1:-1, 1:-1, 1:] - full[:, 1:-1, 1:-1, :-1])
    return (
        flux_x[:, :-1]
        - flux_x[:, 1:]
        + (flux_y[:, :, :-1] - flux_y[:, :, 1:])
        + (flux_z[..., :-1] - flux_z[..., 1:])
    )


def gram_of(left, right):
    return jnp.einsum("axyz,bxyz->ab", left, right, precision=lax.Precision.HIGHEST)


def combine_cols(field, matrix):
    return jnp.einsum("axyz,ab->bxyz", field, matrix, precision=lax.Precision.HIGHEST)


def posdef_solve(matrix, right):
    lower = jnp.linalg.cholesky(matrix)
    middle = lax.linalg.triangular_solve(lower, right, left_side=True, lower=True)
    return lax.linalg.triangular_solve(lower, middle, left_side=True, lower=True, transpose_a=True)


def one_hot(cells, start, count):
    return (cells[:, None] == start + jnp.arange(count, dtype=jnp.int32)[None, :]).astype(
        jnp.float32
    )


def face_terms(field_pad, adjoint_pad):
    fu = jnp.pad(field_pad, ((0, 0), (0, 0), (0, 0), (1, 1)))
    fl = jnp.pad(adjoint_pad, ((0, 0), (0, 0), (0, 0), (1, 1)))
    term_x = jnp.sum(
        (fu[:, 1:, 1:-1, 1:-1] - fu[:, :-1, 1:-1, 1:-1])
        * (fl[:, 1:, 1:-1, 1:-1] - fl[:, :-1, 1:-1, 1:-1]),
        axis=0,
    )
    term_y = jnp.sum(
        (fu[:, 1:-1, 1:, 1:-1] - fu[:, 1:-1, :-1, 1:-1])
        * (fl[:, 1:-1, 1:, 1:-1] - fl[:, 1:-1, :-1, 1:-1]),
        axis=0,
    )
    term_z = jnp.sum(
        (fu[:, 1:-1, 1:-1, 1:] - fu[:, 1:-1, 1:-1, :-1])
        * (fl[:, 1:-1, 1:-1, 1:] - fl[:, 1:-1, 1:-1, :-1]),
        axis=0,
    )
    return (term_x, term_y, term_z)


HI = lax.Precision.HIGHEST

def _mm(a, b):
    return jnp.dot(a, b, precision=HI, preferred_element_type=jnp.float32)

def _tr(a):
    return jnp.transpose(a)

def _solve(pairs, unroll):
    n = pairs[0][0].shape[0]
    shape = pairs[0][0].shape
    rows = lax.broadcasted_iota(jnp.int32, shape, 0)
    lanes = lax.broadcasted_iota(jnp.int32, shape, 1)
    lane_r = lax.broadcasted_iota(jnp.int32, (1, n), 1)

    def pick_row(x, i):
        return jnp.sum(jnp.where(rows == i, x, 0.0), axis=0, keepdims=True)

    def pick_col(x, i):
        return jnp.sum(jnp.where(lanes == i, x, 0.0), axis=1, keepdims=True)

    def entry(row, i):
        return jnp.sum(jnp.where(lane_r == i, row, 0.0), axis=1, keepdims=True)

    def pair_inverse(a, b, c, d):
        scale = 1.0 / (a * d - b * c)
        return d * scale, -b * scale, -c * scale, a * scale

    def step(k, carry):
        piv = [4 * k + i for i in range(4)]
        out = []
        for m, r in carry:
            row = [pick_row(m, i) for i in piv]
            res = [pick_row(r, i) for i in piv]
            col = [pick_col(m, i) for i in piv]
            ent = [[entry(row[i], piv[j]) for j in range(4)] for i in range(4)]
            w00, w01, w10, w11 = pair_inverse(ent[0][0], ent[0][1], ent[1][0], ent[1][1])

            def lead(x0, x1):
                return w00 * x0 + w01 * x1, w10 * x0 + w11 * x1

            e02, e12 = lead(ent[0][2], ent[1][2])
            e03, e13 = lead(ent[0][3], ent[1][3])
            t22 = ent[2][2] - ent[2][0] * e02 - ent[2][1] * e12
            t23 = ent[2][3] - ent[2][0] * e03 - ent[2][1] * e13
            t32 = ent[3][2] - ent[3][0] * e02 - ent[3][1] * e12
            t33 = ent[3][3] - ent[3][0] * e03 - ent[3][1] * e13
            v00, v01, v10, v11 = pair_inverse(t22, t23, t32, t33)

            def reduce(x):
                x0, x1 = lead(x[0], x[1])
                x2 = x[2] - ent[2][0] * x0 - ent[2][1] * x1
                x3 = x[3] - ent[3][0] * x0 - ent[3][1] * x1
                y2 = v00 * x2 + v01 * x3
                y3 = v10 * x2 + v11 * x3
                y0 = x0 - e02 * y2 - e03 * y3
                y1 = x1 - e12 * y2 - e13 * y3
                return [y0, y1, y2, y3]

            new_m = reduce(row)
            new_r = reduce(res)
            rest_m = m - col[0] * new_m[0] - col[1] * new_m[1] - col[2] * new_m[2] - col[3] * new_m[3]
            rest_r = r - col[0] * new_r[0] - col[1] * new_r[1] - col[2] * new_r[2] - col[3] * new_r[3]
            for i in range(4):
                rest_m = jnp.where(rows == piv[i], new_m[i], rest_m)
                rest_r = jnp.where(rows == piv[i], new_r[i], rest_r)
            out.append((rest_m, rest_r))
        return tuple(out)

    done = lax.fori_loop(0, n // 4, step, tuple(pairs), unroll=unroll)
    return [r for _, r in done]


def steps_kernel(grams_ref, out_ref):
    g_rr = grams_ref[0]
    g_rq = grams_ref[1]
    g_qq = grams_ref[2]
    g_qw = grams_ref[3]
    n = g_rr.shape[0]
    eye = (
        lax.broadcasted_iota(jnp.int32, (n, n), 0) == lax.broadcasted_iota(jnp.int32, (n, n), 1)
    ).astype(jnp.float32)
    step0, rr_inv = _solve([(g_rq, g_rr), (g_rr, eye)], True)
    cross = _mm(g_rq, step0)
    step0_t = _tr(step0)
    new_gram = g_rr - cross - _tr(cross) + _mm(step0_t, _mm(g_qq, step0))
    turn = _mm(rr_inv, new_gram)
    keep = eye + turn
    keep_t = _tr(keep)
    curv = (
        _mm(keep_t, _mm(g_rq, keep))
        - _mm(keep_t, _mm(g_qq, step0))
        - _mm(step0_t, _mm(g_qq, keep))
        + _mm(step0_t, _mm(g_qw, step0))
    )
    (step1,) = _solve([(curv, new_gram)], True)
    out_ref[0] = step0 + _mm(keep, step1)
    out_ref[1] = -_mm(step0, step1)


def steps(grams):
    n = grams.shape[1]
    return pl.pallas_call(
        steps_kernel,
        out_shape=jax.ShapeDtypeStruct((2, n, n), jnp.float32),
        cost_estimate=pl.CostEstimate(flops=20_000_000_000, transcendentals=0, bytes_accessed=6 * n * n * 4),
    )(grams)


def on_device(conductivity, electrodes, pair_order, initial_fields, adjoint_fields):
    cells_x, cells_y, cells_z = conductivity.shape
    columns = initial_fields.shape[0]
    total_y = lax.axis_size("gy") * cells_y
    start_x = lax.axis_index("gx") * cells_x
    start_y = lax.axis_index("gy") * cells_y
    picked = jnp.take(electrodes, pair_order, axis=0)

    def point_source(flat):
        xs = flat // (total_y * cells_z)
        ys = flat // cells_z % total_y
        zs = flat % cells_z
        return jnp.einsum(
            "cx,cy,cz->cxyz",
            one_hot(xs, start_x, cells_x),
            one_hot(ys, start_y, cells_y),
            one_hot(zs, 0, cells_z),
        )

    right = INJECT * (point_source(picked[:, 0]) - point_source(picked[:, 1]))
    sides = (("gx", 1), ("gy", 2))
    grid_axes = ("gx", "gy")
    stacked = jnp.concatenate([conductivity[None], initial_fields], axis=0)
    padded = padded_2(stacked, sides, 1)
    conds = conductances(padded[0])
    iter_pad = padded[1:]
    residual = right - operator(iter_pad, conds)
    res_pad = padded_2(residual, sides, 1)
    image = operator(res_pad, conds)
    image_pad = padded_2(image, sides, 1)
    image2 = operator(image_pad, conds)
    image2, adjoint_late = lax.optimization_barrier((image2, adjoint_fields))
    adjoint_pad = padded_2(adjoint_late, sides, 1)
    grams = allsum(
        jnp.stack(
            [
                gram_of(residual, residual),
                gram_of(residual, image),
                gram_of(image, image),
                gram_of(image, image2),
            ]
        ),
        grid_axes,
    )

    solved = steps(grams)
    it2_pad = iter_pad + combine_cols(res_pad, solved[0]) + combine_cols(image_pad, solved[1])
    iterate = it2_pad[:, 1:-1, 1:-1]
    term_x, term_y, term_z = face_terms(it2_pad, adjoint_pad)
    local_grad = (
        -0.5
        / columns
        * (
            term_x[:-1]
            + term_x[1:]
            + term_y[:, :-1]
            + term_y[:, 1:]
            + term_z[..., :-1]
            + term_z[..., 1:]
        )
    )
    groups = lax.axis_size("src")
    share = cells_z // groups
    own = lax.axis_index("src")
    if groups == 2:
        other = 1 - own
        sent = lax.dynamic_slice_in_dim(local_grad, other * share, share, 2)
        got = lax.ppermute(sent, "src", [(0, 1), (1, 0)])
        gradient = lax.dynamic_slice_in_dim(local_grad, own * share, share, 2) + got
    else:
        summed = lax.psum(local_grad, "src")
        gradient = lax.dynamic_slice_in_dim(summed, own * share, share, 2)
    return (iterate, gradient)


def solution(mesh):
    placed = (
        P("gx", "gy", None),
        P(),
        P("src"),
        P("src", "gx", "gy", None),
        P("src", "gx", "gy", None),
    )
    return jax.shard_map(
        on_device,
        mesh=mesh,
        in_specs=placed,
        out_specs=(P("src", "gx", "gy", None), P("gx", "gy", "src")),
        check_vma=False,
    )
```

```python
import jax
import jax.numpy as jnp
from jax import lax
from jax.sharding import PartitionSpec as P
from jax.experimental import pallas as pl

ITERS = 2


INJECT = 4.0


def padded_2(block, sides, width):
    (axis_x, dim_x), (axis_y, dim_y) = sides
    pieces = {}
    for axis, dim in sides:
        count = lax.axis_size(axis)
        place = lax.axis_index(axis)
        forward = [(i, (i + 1) % count) for i in range(count)]
        backward = [(target, source) for source, target in forward]
        top = lax.slice_in_dim(block, block.shape[dim] - width, None, axis=dim)
        bottom = lax.slice_in_dim(block, 0, width, axis=dim)
        top = jnp.where(place == count - 1, jnp.zeros_like(top), top)
        bottom = jnp.where(place == 0, jnp.zeros_like(bottom), bottom)
        low = lax.ppermute(top, axis, forward)
        high = lax.ppermute(bottom, axis, backward)
        pieces[axis] = (low, high)
    low_x, high_x = pieces[axis_x]
    low_y, high_y = pieces[axis_y]
    middle = jnp.concatenate([low_x, block, high_x], axis=dim_x)
    rim = [(0, 0)] * block.ndim
    rim[dim_x] = (width, width)
    low_y = jnp.pad(low_y, rim)
    high_y = jnp.pad(high_y, rim)
    return jnp.concatenate([low_y, middle, high_y], axis=dim_y)


def allsum(value, axes):
    for axis in axes:
        count = lax.axis_size(axis)
        if count & (count - 1):
            value = lax.psum(value, axis)
            continue
        shift = 0
        if (count.bit_length() - 1) % 2:
            value = value + lax.ppermute(value, axis, [(i, i ^ 1) for i in range(count)])
            shift = 1
        while (1 << shift) < count:
            got = [
                lax.ppermute(value, axis, [(i, i ^ (d << shift)) for i in range(count)])
                for d in (1, 2, 3)
            ]
            value = (value + got[0]) + (got[1] + got[2])
            shift += 2
    return value


def conductances(sig_pad):
    full = jnp.pad(sig_pad, ((0, 0), (0, 0), (1, 1)))
    cond_x = 0.5 * (full[1:, 1:-1, 1:-1] + full[:-1, 1:-1, 1:-1])
    cond_y = 0.5 * (full[1:-1, 1:, 1:-1] + full[1:-1, :-1, 1:-1])
    cond_z = 0.5 * (full[1:-1, 1:-1, 1:] + full[1:-1, 1:-1, :-1])
    return (cond_x, cond_y, cond_z)


def operator(padded, conds):
    full = jnp.pad(padded, ((0, 0), (0, 0), (0, 0), (1, 1)))
    flux_x = conds[0] * (full[:, 1:, 1:-1, 1:-1] - full[:, :-1, 1:-1, 1:-1])
    flux_y = conds[1] * (full[:, 1:-1, 1:, 1:-1] - full[:, 1:-1, :-1, 1:-1])
    flux_z = conds[2] * (full[:, 1:-1, 1:-1, 1:] - full[:, 1:-1, 1:-1, :-1])
    return (
        flux_x[:, :-1]
        - flux_x[:, 1:]
        + (flux_y[:, :, :-1] - flux_y[:, :, 1:])
        + (flux_z[..., :-1] - flux_z[..., 1:])
    )


def gram_of(left, right):
    return jnp.einsum("axyz,bxyz->ab", left, right, precision=lax.Precision.HIGHEST)


def combine_cols(field, matrix):
    return jnp.einsum("axyz,ab->bxyz", field, matrix, precision=lax.Precision.HIGHEST)


def posdef_solve(matrix, right):
    lower = jnp.linalg.cholesky(matrix)
    middle = lax.linalg.triangular_solve(lower, right, left_side=True, lower=True)
    return lax.linalg.triangular_solve(lower, middle, left_side=True, lower=True, transpose_a=True)


def one_hot(cells, start, count):
    return (cells[:, None] == start + jnp.arange(count, dtype=jnp.int32)[None, :]).astype(
        jnp.float32
    )


def face_terms(field_pad, adjoint_pad):
    fu = jnp.pad(field_pad, ((0, 0), (0, 0), (0, 0), (1, 1)))
    fl = jnp.pad(adjoint_pad, ((0, 0), (0, 0), (0, 0), (1, 1)))
    term_x = jnp.sum(
        (fu[:, 1:, 1:-1, 1:-1] - fu[:, :-1, 1:-1, 1:-1])
        * (fl[:, 1:, 1:-1, 1:-1] - fl[:, :-1, 1:-1, 1:-1]),
        axis=0,
    )
    term_y = jnp.sum(
        (fu[:, 1:-1, 1:, 1:-1] - fu[:, 1:-1, :-1, 1:-1])
        * (fl[:, 1:-1, 1:, 1:-1] - fl[:, 1:-1, :-1, 1:-1]),
        axis=0,
    )
    term_z = jnp.sum(
        (fu[:, 1:-1, 1:-1, 1:] - fu[:, 1:-1, 1:-1, :-1])
        * (fl[:, 1:-1, 1:-1, 1:] - fl[:, 1:-1, 1:-1, :-1]),
        axis=0,
    )
    return (term_x, term_y, term_z)


HI = lax.Precision.HIGHEST

def _mm(a, b):
    return jnp.dot(a, b, precision=HI, preferred_element_type=jnp.float32)

def _tr(a):
    return jnp.transpose(a)

def _solve(pairs, unroll):
    n = pairs[0][0].shape[0]
    shape = pairs[0][0].shape
    rows = lax.broadcasted_iota(jnp.int32, shape, 0)
    lanes = lax.broadcasted_iota(jnp.int32, shape, 1)
    lane_r = lax.broadcasted_iota(jnp.int32, (1, n), 1)

    def pick_row(x, i):
        return jnp.sum(jnp.where(rows == i, x, 0.0), axis=0, keepdims=True)

    def pick_col(x, i):
        return jnp.sum(jnp.where(lanes == i, x, 0.0), axis=1, keepdims=True)

    def entry(row, i):
        return jnp.sum(jnp.where(lane_r == i, row, 0.0), axis=1, keepdims=True)

    def pair_inverse(a, b, c, d):
        scale = 1.0 / (a * d - b * c)
        return d * scale, -b * scale, -c * scale, a * scale

    def step(k, carry):
        piv = [4 * k + i for i in range(4)]
        out = []
        for m, r in carry:
            row = [pick_row(m, i) for i in piv]
            res = [pick_row(r, i) for i in piv]
            col = [pick_col(m, i) for i in piv]
            ent = [[entry(row[i], piv[j]) for j in range(4)] for i in range(4)]
            w00, w01, w10, w11 = pair_inverse(ent[0][0], ent[0][1], ent[1][0], ent[1][1])

            def lead(x0, x1):
                return w00 * x0 + w01 * x1, w10 * x0 + w11 * x1

            e02, e12 = lead(ent[0][2], ent[1][2])
            e03, e13 = lead(ent[0][3], ent[1][3])
            t22 = ent[2][2] - ent[2][0] * e02 - ent[2][1] * e12
            t23 = ent[2][3] - ent[2][0] * e03 - ent[2][1] * e13
            t32 = ent[3][2] - ent[3][0] * e02 - ent[3][1] * e12
            t33 = ent[3][3] - ent[3][0] * e03 - ent[3][1] * e13
            v00, v01, v10, v11 = pair_inverse(t22, t23, t32, t33)

            def reduce(x):
                x0, x1 = lead(x[0], x[1])
                x2 = x[2] - ent[2][0] * x0 - ent[2][1] * x1
                x3 = x[3] - ent[3][0] * x0 - ent[3][1] * x1
                y2 = v00 * x2 + v01 * x3
                y3 = v10 * x2 + v11 * x3
                y0 = x0 - e02 * y2 - e03 * y3
                y1 = x1 - e12 * y2 - e13 * y3
                return [y0, y1, y2, y3]

            new_m = reduce(row)
            new_r = reduce(res)
            rest_m = m - col[0] * new_m[0] - col[1] * new_m[1] - col[2] * new_m[2] - col[3] * new_m[3]
            rest_r = r - col[0] * new_r[0] - col[1] * new_r[1] - col[2] * new_r[2] - col[3] * new_r[3]
            for i in range(4):
                rest_m = jnp.where(rows == piv[i], new_m[i], rest_m)
                rest_r = jnp.where(rows == piv[i], new_r[i], rest_r)
            out.append((rest_m, rest_r))
        return tuple(out)

    done = lax.fori_loop(0, n // 4, step, tuple(pairs), unroll=unroll)
    return [r for _, r in done]


def steps_kernel(grams_ref, out_ref):
    g_rr = grams_ref[0]
    g_rq = grams_ref[1]
    g_qq = grams_ref[2]
    g_qw = grams_ref[3]
    n = g_rr.shape[0]
    eye = (
        lax.broadcasted_iota(jnp.int32, (n, n), 0) == lax.broadcasted_iota(jnp.int32, (n, n), 1)
    ).astype(jnp.float32)
    step0, rr_inv = _solve([(g_rq, g_rr), (g_rr, eye)], True)
    cross = _mm(g_rq, step0)
    step0_t = _tr(step0)
    new_gram = g_rr - cross - _tr(cross) + _mm(step0_t, _mm(g_qq, step0))
    turn = _mm(rr_inv, new_gram)
    keep = eye + turn
    keep_t = _tr(keep)
    curv = _mm(keep_t, _mm(g_rq, keep) - _mm(g_qq, step0)) + _mm(
        step0_t, _mm(g_qw, step0) - _mm(g_qq, keep)
    )
    (step1,) = _solve([(curv, new_gram)], True)
    out_ref[0] = step0 + _mm(keep, step1)
    out_ref[1] = -_mm(step0, step1)


def steps(grams):
    n = grams.shape[1]
    return pl.pallas_call(
        steps_kernel,
        out_shape=jax.ShapeDtypeStruct((2, n, n), jnp.float32),
        cost_estimate=pl.CostEstimate(flops=20_000_000_000, transcendentals=0, bytes_accessed=6 * n * n * 4),
    )(grams)


def on_device(conductivity, electrodes, pair_order, initial_fields, adjoint_fields):
    cells_x, cells_y, cells_z = conductivity.shape
    columns = initial_fields.shape[0]
    total_y = lax.axis_size("gy") * cells_y
    start_x = lax.axis_index("gx") * cells_x
    start_y = lax.axis_index("gy") * cells_y
    picked = jnp.take(electrodes, pair_order, axis=0)

    def point_source(flat):
        xs = flat // (total_y * cells_z)
        ys = flat // cells_z % total_y
        zs = flat % cells_z
        return jnp.einsum(
            "cx,cy,cz->cxyz",
            one_hot(xs, start_x, cells_x),
            one_hot(ys, start_y, cells_y),
            one_hot(zs, 0, cells_z),
        )

    right = INJECT * (point_source(picked[:, 0]) - point_source(picked[:, 1]))
    sides = (("gx", 1), ("gy", 2))
    grid_axes = ("gx", "gy")
    stacked = jnp.concatenate([conductivity[None], initial_fields], axis=0)
    padded = padded_2(stacked, sides, 1)
    conds = conductances(padded[0])
    iter_pad = padded[1:]
    residual = right - operator(iter_pad, conds)
    res_pad = padded_2(residual, sides, 1)
    image = operator(res_pad, conds)
    image_pad = padded_2(image, sides, 1)
    image2 = operator(image_pad, conds)
    image2, adjoint_late = lax.optimization_barrier((image2, adjoint_fields))
    adjoint_pad = padded_2(adjoint_late, sides, 1)
    grams = allsum(
        jnp.stack(
            [
                gram_of(residual, residual),
                gram_of(residual, image),
                gram_of(image, image),
                gram_of(image, image2),
            ]
        ),
        grid_axes,
    )

    solved = steps(grams)
    it2_pad = iter_pad + combine_cols(res_pad, solved[0]) + combine_cols(image_pad, solved[1])
    iterate = it2_pad[:, 1:-1, 1:-1]
    term_x, term_y, term_z = face_terms(it2_pad, adjoint_pad)
    local_grad = (
        -0.5
        / columns
        * (
            term_x[:-1]
            + term_x[1:]
            + term_y[:, :-1]
            + term_y[:, 1:]
            + term_z[..., :-1]
            + term_z[..., 1:]
        )
    )
    groups = lax.axis_size("src")
    share = cells_z // groups
    own = lax.axis_index("src")
    if groups == 2:
        other = 1 - own
        sent = lax.dynamic_slice_in_dim(local_grad, other * share, share, 2)
        got = lax.ppermute(sent, "src", [(0, 1), (1, 0)])
        gradient = lax.dynamic_slice_in_dim(local_grad, own * share, share, 2) + got
    else:
        summed = lax.psum(local_grad, "src")
        gradient = lax.dynamic_slice_in_dim(summed, own * share, share, 2)
    return (iterate, gradient)


def solution(mesh):
    placed = (
        P("gx", "gy", None),
        P(),
        P("src"),
        P("src", "gx", "gy", None),
        P("src", "gx", "gy", None),
    )
    return jax.shard_map(
        on_device,
        mesh=mesh,
        in_specs=placed,
        out_specs=(P("src", "gx", "gy", None), P("gx", "gy", "src")),
        check_vma=False,
    )
```

```python
import jax
import jax.numpy as jnp
from jax import lax
from jax.sharding import PartitionSpec as P
from jax.experimental import pallas as pl

ITERS = 2


INJECT = 4.0


def padded_2(block, sides, width):
    (axis_x, dim_x), (axis_y, dim_y) = sides
    pieces = {}
    for axis, dim in sides:
        count = lax.axis_size(axis)
        place = lax.axis_index(axis)
        forward = [(i, (i + 1) % count) for i in range(count)]
        backward = [(target, source) for source, target in forward]
        top = lax.slice_in_dim(block, block.shape[dim] - width, None, axis=dim)
        bottom = lax.slice_in_dim(block, 0, width, axis=dim)
        top = jnp.where(place == count - 1, jnp.zeros_like(top), top)
        bottom = jnp.where(place == 0, jnp.zeros_like(bottom), bottom)
        low = lax.ppermute(top, axis, forward)
        high = lax.ppermute(bottom, axis, backward)
        pieces[axis] = (low, high)
    low_x, high_x = pieces[axis_x]
    low_y, high_y = pieces[axis_y]
    middle = jnp.concatenate([low_x, block, high_x], axis=dim_x)
    rim = [(0, 0)] * block.ndim
    rim[dim_x] = (width, width)
    low_y = jnp.pad(low_y, rim)
    high_y = jnp.pad(high_y, rim)
    return jnp.concatenate([low_y, middle, high_y], axis=dim_y)


def allsum(value, axes):
    for axis in axes:
        count = lax.axis_size(axis)
        if count & (count - 1):
            value = lax.psum(value, axis)
            continue
        shift = 0
        if (count.bit_length() - 1) % 2:
            value = value + lax.ppermute(value, axis, [(i, i ^ 1) for i in range(count)])
            shift = 1
        while (1 << shift) < count:
            got = [
                lax.ppermute(value, axis, [(i, i ^ (d << shift)) for i in range(count)])
                for d in (1, 2, 3)
            ]
            value = (value + got[0]) + (got[1] + got[2])
            shift += 2
    return value


def conductances(sig_pad):
    full = jnp.pad(sig_pad, ((0, 0), (0, 0), (1, 1)))
    cond_x = 0.5 * (full[1:, 1:-1, 1:-1] + full[:-1, 1:-1, 1:-1])
    cond_y = 0.5 * (full[1:-1, 1:, 1:-1] + full[1:-1, :-1, 1:-1])
    cond_z = 0.5 * (full[1:-1, 1:-1, 1:] + full[1:-1, 1:-1, :-1])
    return (cond_x, cond_y, cond_z)


def operator(padded, conds):
    full = jnp.pad(padded, ((0, 0), (0, 0), (0, 0), (1, 1)))
    flux_x = conds[0] * (full[:, 1:, 1:-1, 1:-1] - full[:, :-1, 1:-1, 1:-1])
    flux_y = conds[1] * (full[:, 1:-1, 1:, 1:-1] - full[:, 1:-1, :-1, 1:-1])
    flux_z = conds[2] * (full[:, 1:-1, 1:-1, 1:] - full[:, 1:-1, 1:-1, :-1])
    return (
        flux_x[:, :-1]
        - flux_x[:, 1:]
        + (flux_y[:, :, :-1] - flux_y[:, :, 1:])
        + (flux_z[..., :-1] - flux_z[..., 1:])
    )


def gram_of(left, right):
    return jnp.einsum("axyz,bxyz->ab", left, right, precision=lax.Precision.HIGHEST)


def combine_cols(field, matrix):
    return jnp.einsum("axyz,ab->bxyz", field, matrix, precision=lax.Precision.HIGHEST)


def posdef_solve(matrix, right):
    lower = jnp.linalg.cholesky(matrix)
    middle = lax.linalg.triangular_solve(lower, right, left_side=True, lower=True)
    return lax.linalg.triangular_solve(lower, middle, left_side=True, lower=True, transpose_a=True)


def one_hot(cells, start, count):
    return (cells[:, None] == start + jnp.arange(count, dtype=jnp.int32)[None, :]).astype(
        jnp.float32
    )


def face_terms(field_pad, adjoint_pad):
    fu = jnp.pad(field_pad, ((0, 0), (0, 0), (0, 0), (1, 1)))
    fl = jnp.pad(adjoint_pad, ((0, 0), (0, 0), (0, 0), (1, 1)))
    term_x = jnp.sum(
        (fu[:, 1:, 1:-1, 1:-1] - fu[:, :-1, 1:-1, 1:-1])
        * (fl[:, 1:, 1:-1, 1:-1] - fl[:, :-1, 1:-1, 1:-1]),
        axis=0,
    )
    term_y = jnp.sum(
        (fu[:, 1:-1, 1:, 1:-1] - fu[:, 1:-1, :-1, 1:-1])
        * (fl[:, 1:-1, 1:, 1:-1] - fl[:, 1:-1, :-1, 1:-1]),
        axis=0,
    )
    term_z = jnp.sum(
        (fu[:, 1:-1, 1:-1, 1:] - fu[:, 1:-1, 1:-1, :-1])
        * (fl[:, 1:-1, 1:-1, 1:] - fl[:, 1:-1, 1:-1, :-1]),
        axis=0,
    )
    return (term_x, term_y, term_z)


HI = lax.Precision.HIGHEST

def _mm(a, b):
    return jnp.dot(a, b, precision=HI, preferred_element_type=jnp.float32)

def _tr(a):
    return jnp.transpose(a)

def _solve(pairs, unroll):
    n = pairs[0][0].shape[0]
    shape = pairs[0][0].shape
    rows = lax.broadcasted_iota(jnp.int32, shape, 0)
    lanes = lax.broadcasted_iota(jnp.int32, shape, 1)
    lane_r = lax.broadcasted_iota(jnp.int32, (1, n), 1)

    def pick_row(x, i):
        return jnp.sum(jnp.where(rows == i, x, 0.0), axis=0, keepdims=True)

    def pick_col(x, i):
        return jnp.sum(jnp.where(lanes == i, x, 0.0), axis=1, keepdims=True)

    def entry(row, i):
        return jnp.sum(jnp.where(lane_r == i, row, 0.0), axis=1, keepdims=True)

    def pair_inverse(a, b, c, d):
        scale = 1.0 / (a * d - b * c)
        return d * scale, -b * scale, -c * scale, a * scale

    def step(k, carry):
        piv = [4 * k + i for i in range(4)]
        out = []
        for m, r in carry:
            row = [pick_row(m, i) for i in piv]
            res = [pick_row(r, i) for i in piv]
            col = [pick_col(m, i) for i in piv]
            ent = [[entry(row[i], piv[j]) for j in range(4)] for i in range(4)]
            w00, w01, w10, w11 = pair_inverse(ent[0][0], ent[0][1], ent[1][0], ent[1][1])

            def lead(x0, x1):
                return w00 * x0 + w01 * x1, w10 * x0 + w11 * x1

            e02, e12 = lead(ent[0][2], ent[1][2])
            e03, e13 = lead(ent[0][3], ent[1][3])
            t22 = ent[2][2] - ent[2][0] * e02 - ent[2][1] * e12
            t23 = ent[2][3] - ent[2][0] * e03 - ent[2][1] * e13
            t32 = ent[3][2] - ent[3][0] * e02 - ent[3][1] * e12
            t33 = ent[3][3] - ent[3][0] * e03 - ent[3][1] * e13
            v00, v01, v10, v11 = pair_inverse(t22, t23, t32, t33)

            def reduce(x):
                x0, x1 = lead(x[0], x[1])
                x2 = x[2] - ent[2][0] * x0 - ent[2][1] * x1
                x3 = x[3] - ent[3][0] * x0 - ent[3][1] * x1
                y2 = v00 * x2 + v01 * x3
                y3 = v10 * x2 + v11 * x3
                y0 = x0 - e02 * y2 - e03 * y3
                y1 = x1 - e12 * y2 - e13 * y3
                return [y0, y1, y2, y3]

            new_m = reduce(row)
            new_r = reduce(res)
            rest_m = m - col[0] * new_m[0] - col[1] * new_m[1] - col[2] * new_m[2] - col[3] * new_m[3]
            rest_r = r - col[0] * new_r[0] - col[1] * new_r[1] - col[2] * new_r[2] - col[3] * new_r[3]
            for i in range(4):
                rest_m = jnp.where(rows == piv[i], new_m[i], rest_m)
                rest_r = jnp.where(rows == piv[i], new_r[i], rest_r)
            out.append((rest_m, rest_r))
        return tuple(out)

    done = lax.fori_loop(0, n // 4, step, tuple(pairs), unroll=unroll)
    return [r for _, r in done]


def steps_kernel(grams_ref, out_ref):
    g_rr = grams_ref[0]
    g_rq = grams_ref[1]
    g_qq = grams_ref[2]
    g_qw = grams_ref[3]
    n = g_rr.shape[0]
    eye = (
        lax.broadcasted_iota(jnp.int32, (n, n), 0) == lax.broadcasted_iota(jnp.int32, (n, n), 1)
    ).astype(jnp.float32)
    step0, rr_inv = _solve([(g_rq, g_rr), (g_rr, eye)], True)
    cross = _mm(g_rq, step0)
    step0_t = _tr(step0)
    new_gram = g_rr - cross - _tr(cross) + _mm(step0_t, _mm(g_qq, step0))
    turn = _mm(rr_inv, new_gram)
    keep = eye + turn
    keep_t = _tr(keep)
    curv = _mm(keep_t, _mm(g_rq, keep) - _mm(g_qq, step0)) + _mm(
        step0_t, _mm(g_qw, step0) - _mm(g_qq, keep)
    )
    (step1,) = _solve([(curv, new_gram)], True)
    out_ref[0] = step0 + _mm(keep, step1)
    out_ref[1] = -_mm(step0, step1)


def steps(grams):
    n = grams.shape[1]
    return pl.pallas_call(
        steps_kernel,
        out_shape=jax.ShapeDtypeStruct((2, n, n), jnp.float32),
        cost_estimate=pl.CostEstimate(flops=20_000_000_000, transcendentals=0, bytes_accessed=6 * n * n * 4),
    )(grams)


def on_device(conductivity, electrodes, pair_order, initial_fields, adjoint_fields):
    cells_x, cells_y, cells_z = conductivity.shape
    columns = initial_fields.shape[0]
    total_y = lax.axis_size("gy") * cells_y
    start_x = lax.axis_index("gx") * cells_x
    start_y = lax.axis_index("gy") * cells_y
    picked = jnp.take(electrodes, pair_order, axis=0)

    def point_source(flat):
        xs = flat // (total_y * cells_z)
        ys = flat // cells_z % total_y
        zs = flat % cells_z
        return jnp.einsum(
            "cx,cy,cz->cxyz",
            one_hot(xs, start_x, cells_x),
            one_hot(ys, start_y, cells_y),
            one_hot(zs, 0, cells_z),
        )

    right = INJECT * (point_source(picked[:, 0]) - point_source(picked[:, 1]))
    sides = (("gx", 1), ("gy", 2))
    grid_axes = ("gx", "gy")
    stacked = jnp.concatenate([conductivity[None], initial_fields], axis=0)
    padded = padded_2(stacked, sides, 1)
    conds = conductances(padded[0])
    iter_pad = padded[1:]
    residual = right - operator(iter_pad, conds)
    res_pad = padded_2(residual, sides, 1)
    image = operator(res_pad, conds)
    image_pad = padded_2(image, sides, 1)
    image2 = operator(image_pad, conds)
    image2, adjoint_late = lax.optimization_barrier((image2, adjoint_fields))
    adjoint_pad = padded_2(adjoint_late, sides, 1)
    grams = allsum(
        jnp.stack(
            [
                gram_of(residual, residual),
                gram_of(residual, image),
                gram_of(image, image),
                gram_of(image, image2),
            ]
        ),
        grid_axes,
    )

    solved = steps(grams)
    def combine_high(field, matrix):
        return jnp.einsum("axyz,ab->bxyz", field, matrix, precision=lax.Precision.HIGH)

    it2_pad = iter_pad + combine_high(res_pad, solved[0]) + combine_high(image_pad, solved[1])
    iterate = it2_pad[:, 1:-1, 1:-1]
    term_x, term_y, term_z = face_terms(it2_pad, adjoint_pad)
    local_grad = (
        -0.5
        / columns
        * (
            term_x[:-1]
            + term_x[1:]
            + term_y[:, :-1]
            + term_y[:, 1:]
            + term_z[..., :-1]
            + term_z[..., 1:]
        )
    )
    groups = lax.axis_size("src")
    share = cells_z // groups
    own = lax.axis_index("src")
    if groups == 2:
        other = 1 - own
        sent = lax.dynamic_slice_in_dim(local_grad, other * share, share, 2)
        got = lax.ppermute(sent, "src", [(0, 1), (1, 0)])
        gradient = lax.dynamic_slice_in_dim(local_grad, own * share, share, 2) + got
    else:
        summed = lax.psum(local_grad, "src")
        gradient = lax.dynamic_slice_in_dim(summed, own * share, share, 2)
    return (iterate, gradient)


def solution(mesh):
    placed = (
        P("gx", "gy", None),
        P(),
        P("src"),
        P("src", "gx", "gy", None),
        P("src", "gx", "gy", None),
    )
    return jax.shard_map(
        on_device,
        mesh=mesh,
        in_specs=placed,
        out_specs=(P("src", "gx", "gy", None), P("gx", "gy", "src")),
        check_vma=False,
    )
```

```python
import jax
import jax.numpy as jnp
from jax import lax
from jax.sharding import PartitionSpec as P
from jax.experimental import pallas as pl

ITERS = 2


INJECT = 4.0


def padded_2(block, sides, width):
    (axis_x, dim_x), (axis_y, dim_y) = sides
    pieces = {}
    for axis, dim in sides:
        count = lax.axis_size(axis)
        place = lax.axis_index(axis)
        forward = [(i, (i + 1) % count) for i in range(count)]
        backward = [(target, source) for source, target in forward]
        top = lax.slice_in_dim(block, block.shape[dim] - width, None, axis=dim)
        bottom = lax.slice_in_dim(block, 0, width, axis=dim)
        top = jnp.where(place == count - 1, jnp.zeros_like(top), top)
        bottom = jnp.where(place == 0, jnp.zeros_like(bottom), bottom)
        low = lax.ppermute(top, axis, forward)
        high = lax.ppermute(bottom, axis, backward)
        pieces[axis] = (low, high)
    low_x, high_x = pieces[axis_x]
    low_y, high_y = pieces[axis_y]
    middle = jnp.concatenate([low_x, block, high_x], axis=dim_x)
    rim = [(0, 0)] * block.ndim
    rim[dim_x] = (width, width)
    low_y = jnp.pad(low_y, rim)
    high_y = jnp.pad(high_y, rim)
    return jnp.concatenate([low_y, middle, high_y], axis=dim_y)


def allsum(value, axes):
    for axis in axes:
        count = lax.axis_size(axis)
        if count & (count - 1):
            value = lax.psum(value, axis)
            continue
        shift = 0
        if (count.bit_length() - 1) % 2:
            value = value + lax.ppermute(value, axis, [(i, i ^ 1) for i in range(count)])
            shift = 1
        while (1 << shift) < count:
            got = [
                lax.ppermute(value, axis, [(i, i ^ (d << shift)) for i in range(count)])
                for d in (1, 2, 3)
            ]
            value = (value + got[0]) + (got[1] + got[2])
            shift += 2
    return value


def conductances(sig_pad):
    full = jnp.pad(sig_pad, ((0, 0), (0, 0), (1, 1)))
    cond_x = 0.5 * (full[1:, 1:-1, 1:-1] + full[:-1, 1:-1, 1:-1])
    cond_y = 0.5 * (full[1:-1, 1:, 1:-1] + full[1:-1, :-1, 1:-1])
    cond_z = 0.5 * (full[1:-1, 1:-1, 1:] + full[1:-1, 1:-1, :-1])
    return (cond_x, cond_y, cond_z)


def operator(padded, conds):
    full = jnp.pad(padded, ((0, 0), (0, 0), (0, 0), (1, 1)))
    flux_x = conds[0] * (full[:, 1:, 1:-1, 1:-1] - full[:, :-1, 1:-1, 1:-1])
    flux_y = conds[1] * (full[:, 1:-1, 1:, 1:-1] - full[:, 1:-1, :-1, 1:-1])
    flux_z = conds[2] * (full[:, 1:-1, 1:-1, 1:] - full[:, 1:-1, 1:-1, :-1])
    return (
        flux_x[:, :-1]
        - flux_x[:, 1:]
        + (flux_y[:, :, :-1] - flux_y[:, :, 1:])
        + (flux_z[..., :-1] - flux_z[..., 1:])
    )


def gram_of(left, right):
    return jnp.einsum("axyz,bxyz->ab", left, right, precision=lax.Precision.HIGHEST)


def combine_cols(field, matrix):
    return jnp.einsum("axyz,ab->bxyz", field, matrix, precision=lax.Precision.HIGHEST)


def posdef_solve(matrix, right):
    lower = jnp.linalg.cholesky(matrix)
    middle = lax.linalg.triangular_solve(lower, right, left_side=True, lower=True)
    return lax.linalg.triangular_solve(lower, middle, left_side=True, lower=True, transpose_a=True)


def one_hot(cells, start, count):
    return (cells[:, None] == start + jnp.arange(count, dtype=jnp.int32)[None, :]).astype(
        jnp.float32
    )


def face_terms(field_pad, adjoint_pad):
    fu = jnp.pad(field_pad, ((0, 0), (0, 0), (0, 0), (1, 1)))
    fl = jnp.pad(adjoint_pad, ((0, 0), (0, 0), (0, 0), (1, 1)))
    term_x = jnp.sum(
        (fu[:, 1:, 1:-1, 1:-1] - fu[:, :-1, 1:-1, 1:-1])
        * (fl[:, 1:, 1:-1, 1:-1] - fl[:, :-1, 1:-1, 1:-1]),
        axis=0,
    )
    term_y = jnp.sum(
        (fu[:, 1:-1, 1:, 1:-1] - fu[:, 1:-1, :-1, 1:-1])
        * (fl[:, 1:-1, 1:, 1:-1] - fl[:, 1:-1, :-1, 1:-1]),
        axis=0,
    )
    term_z = jnp.sum(
        (fu[:, 1:-1, 1:-1, 1:] - fu[:, 1:-1, 1:-1, :-1])
        * (fl[:, 1:-1, 1:-1, 1:] - fl[:, 1:-1, 1:-1, :-1]),
        axis=0,
    )
    return (term_x, term_y, term_z)


HI = lax.Precision.HIGHEST

def _mm(a, b):
    return jnp.dot(a, b, precision=HI, preferred_element_type=jnp.float32)

def _tr(a):
    return jnp.transpose(a)

def _solve(pairs, unroll):
    n = pairs[0][0].shape[0]
    shape = pairs[0][0].shape
    rows = lax.broadcasted_iota(jnp.int32, shape, 0)
    lanes = lax.broadcasted_iota(jnp.int32, shape, 1)
    lane_r = lax.broadcasted_iota(jnp.int32, (1, n), 1)

    def pick_row(x, i):
        return jnp.sum(jnp.where(rows == i, x, 0.0), axis=0, keepdims=True)

    def pick_col(x, i):
        return jnp.sum(jnp.where(lanes == i, x, 0.0), axis=1, keepdims=True)

    def entry(row, i):
        return jnp.sum(jnp.where(lane_r == i, row, 0.0), axis=1, keepdims=True)

    def pair_inverse(a, b, c, d):
        scale = 1.0 / (a * d - b * c)
        return d * scale, -b * scale, -c * scale, a * scale

    def step(k, carry):
        piv = [4 * k + i for i in range(4)]
        out = []
        for m, r in carry:
            row = [pick_row(m, i) for i in piv]
            res = [pick_row(r, i) for i in piv]
            col = [pick_col(m, i) for i in piv]
            ent = [[entry(row[i], piv[j]) for j in range(4)] for i in range(4)]
            w00, w01, w10, w11 = pair_inverse(ent[0][0], ent[0][1], ent[1][0], ent[1][1])

            def lead(x0, x1):
                return w00 * x0 + w01 * x1, w10 * x0 + w11 * x1

            e02, e12 = lead(ent[0][2], ent[1][2])
            e03, e13 = lead(ent[0][3], ent[1][3])
            t22 = ent[2][2] - ent[2][0] * e02 - ent[2][1] * e12
            t23 = ent[2][3] - ent[2][0] * e03 - ent[2][1] * e13
            t32 = ent[3][2] - ent[3][0] * e02 - ent[3][1] * e12
            t33 = ent[3][3] - ent[3][0] * e03 - ent[3][1] * e13
            v00, v01, v10, v11 = pair_inverse(t22, t23, t32, t33)

            def reduce(x):
                x0, x1 = lead(x[0], x[1])
                x2 = x[2] - ent[2][0] * x0 - ent[2][1] * x1
                x3 = x[3] - ent[3][0] * x0 - ent[3][1] * x1
                y2 = v00 * x2 + v01 * x3
                y3 = v10 * x2 + v11 * x3
                y0 = x0 - e02 * y2 - e03 * y3
                y1 = x1 - e12 * y2 - e13 * y3
                return [y0, y1, y2, y3]

            new_m = reduce(row)
            new_r = reduce(res)
            rest_m = m - col[0] * new_m[0] - col[1] * new_m[1] - col[2] * new_m[2] - col[3] * new_m[3]
            rest_r = r - col[0] * new_r[0] - col[1] * new_r[1] - col[2] * new_r[2] - col[3] * new_r[3]
            for i in range(4):
                rest_m = jnp.where(rows == piv[i], new_m[i], rest_m)
                rest_r = jnp.where(rows == piv[i], new_r[i], rest_r)
            out.append((rest_m, rest_r))
        return tuple(out)

    done = lax.fori_loop(0, n // 4, step, tuple(pairs), unroll=unroll)
    return [r for _, r in done]


def steps_kernel(grams_ref, out_ref):
    g_rr = grams_ref[0]
    g_rq = grams_ref[1]
    g_qq = grams_ref[2]
    g_qw = grams_ref[3]
    n = g_rr.shape[0]
    eye = (
        lax.broadcasted_iota(jnp.int32, (n, n), 0) == lax.broadcasted_iota(jnp.int32, (n, n), 1)
    ).astype(jnp.float32)
    step0, rr_inv = _solve([(g_rq, g_rr), (g_rr, eye)], True)
    cross = _mm(g_rq, step0)
    step0_t = _tr(step0)
    new_gram = g_rr - cross - _tr(cross) + _mm(step0_t, _mm(g_qq, step0))
    turn = _mm(rr_inv, new_gram)
    keep = eye + turn
    keep_t = _tr(keep)
    curv = _mm(keep_t, _mm(g_rq, keep) - _mm(g_qq, step0)) + _mm(
        step0_t, _mm(g_qw, step0) - _mm(g_qq, keep)
    )
    (step1,) = _solve([(curv, new_gram)], True)
    out_ref[0] = step0 + _mm(keep, step1)
    out_ref[1] = -_mm(step0, step1)


def steps(grams):
    n = grams.shape[1]
    return pl.pallas_call(
        steps_kernel,
        out_shape=jax.ShapeDtypeStruct((2, n, n), jnp.float32),
        cost_estimate=pl.CostEstimate(flops=20_000_000_000, transcendentals=0, bytes_accessed=6 * n * n * 4),
    )(grams)


def on_device(conductivity, electrodes, pair_order, initial_fields, adjoint_fields):
    cells_x, cells_y, cells_z = conductivity.shape
    columns = initial_fields.shape[0]
    total_y = lax.axis_size("gy") * cells_y
    start_x = lax.axis_index("gx") * cells_x
    start_y = lax.axis_index("gy") * cells_y
    picked = jnp.take(electrodes, pair_order, axis=0)

    def point_source(flat):
        xs = flat // (total_y * cells_z)
        ys = flat // cells_z % total_y
        zs = flat % cells_z
        return jnp.einsum(
            "cx,cy,cz->cxyz",
            one_hot(xs, start_x, cells_x),
            one_hot(ys, start_y, cells_y),
            one_hot(zs, 0, cells_z),
        )

    right = INJECT * (point_source(picked[:, 0]) - point_source(picked[:, 1]))
    sides = (("gx", 1), ("gy", 2))
    grid_axes = ("gy", "gx")
    stacked = jnp.concatenate([conductivity[None], initial_fields], axis=0)
    padded = padded_2(stacked, sides, 1)
    conds = conductances(padded[0])
    iter_pad = padded[1:]
    residual = right - operator(iter_pad, conds)
    res_pad = padded_2(residual, sides, 1)
    image = operator(res_pad, conds)
    image_pad = padded_2(image, sides, 1)
    image2 = operator(image_pad, conds)
    image2, adjoint_late = lax.optimization_barrier((image2, adjoint_fields))
    adjoint_pad = padded_2(adjoint_late, sides, 1)
    grams = allsum(
        jnp.stack(
            [
                gram_of(residual, residual),
                gram_of(residual, image),
                gram_of(image, image),
                gram_of(image, image2),
            ]
        ),
        grid_axes,
    )

    solved = steps(grams)
    it2_pad = iter_pad + combine_cols(res_pad, solved[0]) + combine_cols(image_pad, solved[1])
    iterate = it2_pad[:, 1:-1, 1:-1]
    term_x, term_y, term_z = face_terms(it2_pad, adjoint_pad)
    local_grad = (
        -0.5
        / columns
        * (
            term_x[:-1]
            + term_x[1:]
            + term_y[:, :-1]
            + term_y[:, 1:]
            + term_z[..., :-1]
            + term_z[..., 1:]
        )
    )
    groups = lax.axis_size("src")
    share = cells_z // groups
    own = lax.axis_index("src")
    if groups == 2:
        other = 1 - own
        sent = lax.dynamic_slice_in_dim(local_grad, other * share, share, 2)
        got = lax.ppermute(sent, "src", [(0, 1), (1, 0)])
        gradient = lax.dynamic_slice_in_dim(local_grad, own * share, share, 2) + got
    else:
        summed = lax.psum(local_grad, "src")
        gradient = lax.dynamic_slice_in_dim(summed, own * share, share, 2)
    return (iterate, gradient)


def solution(mesh):
    placed = (
        P("gx", "gy", None),
        P(),
        P("src"),
        P("src", "gx", "gy", None),
        P("src", "gx", "gy", None),
    )
    return jax.shard_map(
        on_device,
        mesh=mesh,
        in_specs=placed,
        out_specs=(P("src", "gx", "gy", None), P("gx", "gy", "src")),
        check_vma=False,
    )
```
